32 devices in a mesh: groups: 2 (over y), picks: 4 (over z), heads: 4 (over x, core).
Axes of the slice: x: 2, y: 2, z: 4, core: 2. Of those that a mesh axis runs over, the one named last changes fastest.
Arguments:
- coords: float32 [3, 8192], P(None, ('groups', 'picks')), parts along dimension 1, may hold values from -1 to 1
- horizon_ids: int32 [8192], P(('groups', 'picks')), parts along dimension 0, may hold values from 0 to 63
- horizon_levels: float32 [128], P('groups'), parts along dimension 0, may hold values from -2 to 2
- latents: bfloat16 [512, 1024], replicated, may hold values from -960 to 960
- kv_weight: bfloat16 [3072, 2, 1024], P('picks', None, 'heads'), may hold values from -0.109375 to 0.109375
- cross_out: bfloat16 [1024, 1024], P('heads'), may hold values from -0.75 to 0.75
- norm_gains: float32 [2, 1024], replicated, may hold values from 0.1 to 1.9
- self_qkv: bfloat16 [3, 1024, 1024], P(None, None, 'heads'), may hold values from -0.1875 to 0.1875
- self_out: bfloat16 [1024, 1024], P(None, 'heads'), may hold values from -0.1875 to 0.1875
- dec_kv: bfloat16 [2, 1024, 1024], P(None, None, 'heads'), may hold values from -0.1875 to 0.1875
- dec_query: bfloat16 [3072, 1024], P('picks', 'heads'), may hold values from -0.109375 to 0.109375
- readout: float32 [1024], P('heads'), may hold values from -0.1875 to 0.1875
Outputs:
- field: float32 [8192], P(('groups', 'picks')), parts along dimension 0
- latents_out: float32 [1024, 1024], P('groups', 'heads'), parts along dimension 0
- grad_query: float32 [6144, 1024], P(('groups', 'picks'), 'heads'), parts along dimension 0
The draws below stay inside these ranges and needn't reach their ends.
There are 2 independent parts, one for each index of `groups`. The reference program is written for one: setup_inputs(seed, part) draws one part's arguments, and reference() takes and returns one part's arrays. A program takes and returns all parts, laid end to end along the dimension named above; an argument that names none is the same for every part. Nothing has to cross between parts.
All inputs are finite; a program needn't handle non-finite values.
Results may differ from the reference program's by a relative error of at most 0.028.
Values may be sent and summed in bfloat16 or wider, within the bound.
No kernel may reach another device: no remote copies, remote signals or barrier semaphores. Data moves between devices by JAX's collectives and lax.ppermute only.
A program may use at most 64 MiB of HBM per device.

```python
import jax
import jax.numpy as jnp
from jax import lax

D = 1024
HEAD = 128
LAT = 512
BANDS = 512
HORIZONS = 64
TOK_DEV = 1024
TOKENS = 4096
ENC = 3072
HEADS = 8


def draw_latents(key, part):
    base = jnp.clip(jax.random.normal(key, (LAT, D), jnp.float32), -6.0, 6.0)
    return base.astype(jnp.bfloat16)


def place_ends(drawn, stream_key, smallest, high):
    shape = drawn.shape
    spot = [jax.random.randint(jax.random.fold_in(stream_key, axis), (), 0, shape[axis]) for axis in range(len(shape))]
    drawn = drawn.at[tuple(spot)].set(smallest)
    longest = shape.index(max(shape))
    spot[longest] = (spot[longest] + 1) % shape[longest]
    return drawn.at[tuple(spot)].set(high)


def levels(own_key, extent, shards, low, top_value):
    def one(dim, parts):
        draws = jax.random.uniform(jax.random.fold_in(jax.random.fold_in(own_key, 6), dim), (parts,), jnp.float32, low / len(shards), top_value / len(shards))
        return jnp.repeat(jnp.exp(draws), extent[dim] // parts).reshape((-1,) + (1,) * (len(extent) - dim - 1))

    factor_of = one(*shards[0])
    for cut in shards[1:]:
        factor_of = factor_of * one(*cut)
    return factor_of


def bell_draw(stream_key, dims, deviation, limit, shards=(), held_as=jnp.bfloat16):
    array = deviation * jax.random.normal(stream_key, dims, jnp.float32)
    if shards:
        array = array * levels(stream_key, dims, shards, -0.22, 0.18)
    return jnp.clip(array, -limit, limit).astype(held_as)


def setup_inputs(seed: int = 0, part: int = 0) -> dict:
    seeds = jax.random.split(jax.random.key(seed), 13)
    own_keys = jax.random.split(jax.random.fold_in(seeds[12], part), 13)
    coords = jnp.clip(jax.random.uniform(own_keys[0], (3, TOKENS), jnp.float32, -1.0, 1.0) * levels(own_keys[0], (3, TOKENS), ((1, 4),), -0.4, 0.0), -1.0, 1.0)
    horizon_ids = place_ends(jax.random.randint(own_keys[1], (TOKENS,), 0, HORIZONS), jax.random.fold_in(own_keys[1], 1), 0, HORIZONS - 1).astype(jnp.int32)
    horizon_levels = jnp.clip(jax.random.uniform(own_keys[2], (HORIZONS,), jnp.float32, -2.0, 2.0), -2.0, 2.0)
    latents = draw_latents(jax.random.fold_in(seeds[12], 71), part)
    kv_weight = bell_draw(seeds[4], (ENC, 2, D), ENC ** -0.5, 0.109375, ((0, 4), (2, 4)))
    cross_out = bell_draw(seeds[5], (D, D), (D // 16) ** -0.5, 0.75, ((0, 4),))
    norm_gains = jnp.clip(1.0 + 0.18 * jax.random.normal(seeds[6], (2, D), jnp.float32), 0.1, 1.9)
    self_qkv = bell_draw(seeds[7], (3, D, D), D ** -0.5, 0.1875, ((2, 4),))
    self_out = bell_draw(seeds[8], (D, D), D ** -0.5, 0.1875, ((1, 4),))
    dec_kv = bell_draw(seeds[9], (2, D, D), D ** -0.5, 0.1875, ((2, 4),))
    dec_query = bell_draw(seeds[10], (ENC, D), ENC ** -0.5, 0.109375, ((0, 4), (1, 4)))
    readout = bell_draw(seeds[11], (D,), D ** -0.5, 0.1875, ((0, 4),), jnp.float32)
    return {"coords": coords, "horizon_ids": horizon_ids, "horizon_levels": horizon_levels, "latents": latents, "kv_weight": kv_weight, "cross_out": cross_out, "norm_gains": norm_gains, "self_qkv": self_qkv, "self_out": self_out, "dec_kv": dec_kv, "dec_query": dec_query, "readout": readout}


PI = 3.141592653589793
EPS = 1e-06

def encode(coords):
    freq = jnp.linspace(1.0, BANDS / 2.0, BANDS).astype(jnp.float32)
    angle = PI * freq[None, :, None] * coords[:, None, :]
    table = jnp.concatenate([jnp.sin(angle), jnp.cos(angle)], axis=0)
    return table.reshape(6 * BANDS, coords.shape[1]).T.astype(jnp.bfloat16)

def rms_norm(state, gain):
    power = lax.optimization_barrier(jnp.mean(state * state, axis=1, keepdims=True))
    return (state * lax.rsqrt(power + EPS) * gain[None, :]).astype(jnp.bfloat16)

def reference(coords, horizon_ids, horizon_levels, latents, kv_weight, cross_out, norm_gains, self_qkv, self_out, dec_kv, dec_query, readout):
    high = lax.Precision.HIGHEST
    scale = HEAD ** (-0.5)
    blocks = TOKENS // TOK_DEV
    enc = encode(coords)
    keys_vals = jnp.dot(enc, kv_weight.reshape(ENC, 2 * D), preferred_element_type=jnp.float32).astype(jnp.bfloat16)
    keys = keys_vals[:, :D].reshape(TOKENS, HEADS, HEAD).transpose(1, 0, 2)
    values = keys_vals[:, D:].reshape(TOKENS, HEADS, HEAD).transpose(1, 0, 2)
    queries = latents.reshape(LAT, HEADS, HEAD).transpose(1, 0, 2)

    def cross_head(items):
        query_h, key_h, value_h = items
        scores = jnp.dot(query_h, key_h.T, preferred_element_type=jnp.float32) * scale
        scores = scores.reshape(LAT, blocks, TOK_DEV)
        top = lax.optimization_barrier(jnp.max(scores, axis=2))
        expo = jnp.exp(scores - top[:, :, None])
        total = lax.optimization_barrier(jnp.sum(expo, axis=2))
        rounded = lax.optimization_barrier(expo.astype(jnp.bfloat16)).astype(jnp.float32)
        part = jnp.einsum('lbt,btc->lbc', rounded, value_h.reshape(blocks, TOK_DEV, HEAD).astype(jnp.float32), precision=high)
        best = lax.optimization_barrier(jnp.max(top, axis=1, keepdims=True))
        factor = jnp.exp(top - best)
        numer = lax.optimization_barrier(jnp.sum(part * factor[:, :, None], axis=1))
        return numer / lax.optimization_barrier(jnp.sum(total * factor, axis=1))[:, None]
    attended = lax.map(cross_head, (queries, keys, values))
    attended = attended.transpose(1, 0, 2).reshape(LAT, D).astype(jnp.bfloat16)
    state = latents.astype(jnp.float32) + jnp.dot(attended, cross_out, preferred_element_type=jnp.float32)
    normed = rms_norm(state, norm_gains[0])
    qkv = jnp.einsum('ld,kde->kle', normed.astype(jnp.float32), self_qkv.astype(jnp.float32), precision=high).astype(jnp.bfloat16)
    sq = qkv[0].reshape(LAT, HEADS, HEAD).astype(jnp.float32)
    sk = qkv[1].reshape(LAT, HEADS, HEAD).astype(jnp.float32)
    sv = qkv[2].reshape(LAT, HEADS, HEAD).astype(jnp.float32)
    scores = jnp.einsum('lhc,mhc->hlm', sq, sk, precision=high) * scale
    expo = jnp.exp(scores)
    probs = (expo / lax.optimization_barrier(jnp.sum(expo, axis=2, keepdims=True))).astype(jnp.bfloat16)
    head_out = jnp.einsum('hlm,mhc->lhc', probs.astype(jnp.float32), sv, precision=high).astype(jnp.bfloat16).reshape(LAT, D)
    latents_out = state + jnp.dot(head_out, self_out, preferred_element_type=jnp.float32)
    normed2 = rms_norm(latents_out, norm_gains[1])
    dec = jnp.einsum('ld,kde->kle', normed2.astype(jnp.float32), dec_kv.astype(jnp.float32), precision=high).astype(jnp.bfloat16)
    dec_keys = dec[0].reshape(LAT, HEADS, HEAD).astype(jnp.float32)
    dec_vals = dec[1].reshape(LAT, HEADS, HEAD).astype(jnp.float32)
    query = jnp.dot(enc, dec_query, preferred_element_type=jnp.float32).astype(jnp.bfloat16)
    onehot = (horizon_ids[:, None] == jnp.arange(HORIZONS, dtype=jnp.int32)[None, :]).astype(jnp.float32)
    target = lax.optimization_barrier(jnp.sum(onehot * horizon_levels[None, :], axis=1))
    read = readout.reshape(HEADS, HEAD)
    value_read = jnp.einsum('lhc,hc->hl', dec_vals, read, precision=high)

    def decode(items):
        query_b, target_b = items
        dq = query_b.reshape(TOK_DEV, HEADS, HEAD).astype(jnp.float32)
        sc = jnp.einsum('thc,lhc->htl', dq, dec_keys, precision=high) * scale
        ex = jnp.exp(sc)
        weights = ex / lax.optimization_barrier(jnp.sum(ex, axis=2, keepdims=True))
        rounded = lax.optimization_barrier(weights.astype(jnp.bfloat16)).astype(jnp.float32)
        out = jnp.einsum('htl,lhc->thc', rounded, dec_vals, precision=high)
        field_b = lax.optimization_barrier(jnp.sum(out * read[None, :, :], axis=(1, 2)))
        miss = field_b - target_b
        dprob = miss[None, :, None] * value_read[:, None, :]
        dscore = weights * (dprob - lax.optimization_barrier(jnp.sum(dprob * weights, axis=2, keepdims=True)))
        dscore = lax.optimization_barrier(dscore.astype(jnp.bfloat16)).astype(jnp.float32)
        dquery = jnp.einsum('htl,lhc->thc', dscore, dec_keys, precision=high) * scale
        return (field_b, dquery.reshape(TOK_DEV, D).astype(jnp.bfloat16))
    field, dquery = lax.map(decode, (query.reshape(blocks, TOK_DEV, D), target.reshape(blocks, TOK_DEV)))
    grad_query = jnp.dot(enc.T, dquery.reshape(TOKENS, D), preferred_element_type=jnp.float32)
    return (field.reshape(TOKENS), latents_out, grad_query)
```

```python
import functools

import jax
import jax.numpy as jnp
from jax import lax
from jax.sharding import PartitionSpec as P

HEAD = 128
BANDS = 512
HORIZONS = 64


PI = 3.141592653589793
EPS = 1e-06
RING_MAX = 4


def encode(coords):
    freq = jnp.linspace(1.0, BANDS / 2.0, BANDS).astype(jnp.float32)
    angle = PI * freq[None, :, None] * coords[:, None, :]
    table = jnp.concatenate([jnp.sin(angle), jnp.cos(angle)], axis=0)
    return table.reshape(6 * BANDS, coords.shape[1]).T.astype(jnp.bfloat16)


def ring_gather(x, axis, n):
    if n == 1:
        return x
    if n > RING_MAX:
        return lax.all_gather(x, axis, axis=0, tiled=True)
    idx = lax.axis_index(axis)
    blocks = [x]
    for s in range(1, n):
        blocks.append(lax.ppermute(x, axis, [(i, (i - s) % n) for i in range(n)]))
    flipped = jnp.stack(blocks)
    ordered = jnp.roll(flipped, idx, axis=0)
    return ordered.reshape((n * x.shape[0],) + x.shape[1:])


def on_device(
    coords,
    horizon_ids,
    horizon_levels,
    latents,
    kv_weight,
    cross_out,
    norm_gains,
    self_qkv,
    self_out,
    dec_kv,
    dec_query,
    readout,
    *,
    n_picks,
    n_heads,
):
    high = lax.Precision.HIGHEST
    scale = HEAD ** (-0.5)
    count = coords.shape[1]
    width = latents.shape[1]
    lat_rows = latents.shape[0]
    local = kv_weight.shape[2]
    nheads = local // HEAD
    column = lax.axis_index("heads") * local
    enc = encode(coords)
    cross_full = ring_gather(cross_out, "heads", n_heads)
    piece = lax.all_gather(kv_weight, "picks", axis=0, tiled=True)
    keys_vals = jnp.dot(
        enc, piece.reshape(piece.shape[0], 2 * local), preferred_element_type=jnp.float32
    ).astype(jnp.bfloat16)
    keys = keys_vals[:, :local].reshape(count, nheads, HEAD)
    values = keys_vals[:, local:].reshape(count, nheads, HEAD)
    queries = lax.dynamic_slice_in_dim(latents, column, local, 1).reshape(lat_rows, nheads, HEAD)
    scores = jnp.einsum("lhc,thc->hlt", queries, keys, preferred_element_type=jnp.float32) * scale
    top = jnp.max(scores, axis=2)
    expo = jnp.exp(scores - top[:, :, None])
    total = jnp.sum(expo, axis=2)
    numer = jnp.einsum(
        "hlt,thc->hlc", expo.astype(jnp.bfloat16), values, preferred_element_type=jnp.float32
    )
    all_numer = lax.all_gather(numer.astype(jnp.bfloat16), "picks", axis=0, tiled=False)
    all_stats = lax.all_gather(jnp.stack([top, total]), "picks", axis=0, tiled=False)
    best = jnp.max(all_stats[:, 0], axis=0)
    factor = jnp.exp(all_stats[:, 0] - best[None])
    merged_total = jnp.sum(factor * all_stats[:, 1], axis=0)
    merged_numer = jnp.einsum(
        "phl,phlc->hlc", factor, all_numer.astype(jnp.float32), precision=high
    )
    attended = (
        (merged_numer / merged_total[:, :, None])
        .transpose(1, 0, 2)
        .reshape(lat_rows, local)
        .astype(jnp.bfloat16)
    )
    dq_local, attended = lax.optimization_barrier((dec_query, attended))
    dq_full = ring_gather(dq_local, "picks", n_picks)
    gain_two = lax.dynamic_slice_in_dim(norm_gains[1], column, local, 0)
    attended_full = lax.all_gather(attended, "heads", axis=1, tiled=True)
    whole = latents.astype(jnp.float32) + jnp.dot(
        attended_full, cross_full, preferred_element_type=jnp.float32
    )
    power = jnp.mean(whole * whole, axis=1, keepdims=True)
    normed = (whole * lax.rsqrt(power + EPS) * norm_gains[0][None, :]).astype(jnp.bfloat16)
    state = lax.dynamic_slice_in_dim(whole, column, local, 1)
    qkv = jnp.einsum("ld,kde->kle", normed, self_qkv, preferred_element_type=jnp.float32).astype(
        jnp.bfloat16
    )
    self_q = qkv[0].reshape(lat_rows, nheads, HEAD)
    self_k = qkv[1].reshape(lat_rows, nheads, HEAD)
    self_v = qkv[2].reshape(lat_rows, nheads, HEAD)
    inner = jnp.einsum("lhc,mhc->hlm", self_q, self_k, preferred_element_type=jnp.float32) * scale
    raised = jnp.exp(inner)
    probs = (raised / jnp.sum(raised, axis=2, keepdims=True)).astype(jnp.bfloat16)
    head_out = (
        jnp.einsum("hlm,mhc->lhc", probs, self_v, preferred_element_type=jnp.float32)
        .astype(jnp.bfloat16)
        .reshape(lat_rows, local)
    )
    every_head = lax.all_gather(head_out, "heads", axis=1, tiled=True)
    latents_out = state + jnp.dot(every_head, self_out, preferred_element_type=jnp.float32)
    gained = (latents_out * gain_two[None, :]).astype(jnp.bfloat16)
    gained_full = lax.all_gather(gained, "heads", axis=1, tiled=True)
    power_two = lax.psum(jnp.sum(latents_out * latents_out, axis=1), "heads")
    row_scale = lax.rsqrt(power_two / width + EPS)
    dec = (
        jnp.einsum("ld,kde->kle", gained_full, dec_kv, preferred_element_type=jnp.float32)
        * row_scale[None, :, None]
    ).astype(jnp.bfloat16)
    dec_keys = dec[0].reshape(lat_rows, nheads, HEAD)
    dec_vals = dec[1].reshape(lat_rows, nheads, HEAD)
    query = jnp.dot(enc, dq_full, preferred_element_type=jnp.float32).astype(jnp.bfloat16)
    dec_q = query.reshape(count, nheads, HEAD)
    logits = jnp.einsum("thc,lhc->htl", dec_q, dec_keys, preferred_element_type=jnp.float32) * scale
    lifted = jnp.exp(logits)
    weights = lifted / jnp.sum(lifted, axis=2, keepdims=True)
    out = jnp.einsum(
        "htl,lhc->thc", weights.astype(jnp.bfloat16), dec_vals, preferred_element_type=jnp.float32
    )
    read = readout.reshape(nheads, HEAD)
    field = lax.psum(jnp.sum(out * read[None, :, :], axis=(1, 2)), "heads")
    onehot = (horizon_ids[:, None] == jnp.arange(HORIZONS, dtype=jnp.int32)[None, :]).astype(
        jnp.float32
    )
    target = jnp.sum(onehot * horizon_levels[None, :], axis=1)
    miss = field - target
    value_read = jnp.einsum("lhc,hc->hl", dec_vals.astype(jnp.float32), read, precision=high)
    dprob = miss[None, :, None] * value_read[:, None, :]
    dscore = (weights * (dprob - jnp.sum(dprob * weights, axis=2, keepdims=True))).astype(
        jnp.bfloat16
    )
    dquery = (
        (jnp.einsum("htl,lhc->thc", dscore, dec_keys, preferred_element_type=jnp.float32) * scale)
        .reshape(count, local)
        .astype(jnp.bfloat16)
    )
    grad_query = lax.psum_scatter(
        jnp.dot(enc.T, dquery, preferred_element_type=jnp.float32).astype(jnp.bfloat16),
        "picks",
        scatter_dimension=0,
        tiled=True,
    ).astype(jnp.float32)
    return (field, latents_out, grad_query)


def solution(mesh):
    in_specs = (
        P(None, ("groups", "picks")),
        P(("groups", "picks")),
        P("groups"),
        P(),
        P("picks", None, "heads"),
        P("heads", None),
        P(),
        P(None, None, "heads"),
        P(None, "heads"),
        P(None, None, "heads"),
        P("picks", "heads"),
        P("heads"),
    )
    out_specs = (P(("groups", "picks")), P("groups", "heads"), P(("groups", "picks"), "heads"))
    body = functools.partial(
        on_device, n_picks=mesh.shape["picks"], n_heads=mesh.shape["heads"]
    )
    return jax.shard_map(body, mesh=mesh, in_specs=in_specs, out_specs=out_specs, check_vma=False)
```

```python
import functools

import jax
import jax.numpy as jnp
from jax import lax
from jax.sharding import PartitionSpec as P

HEAD = 128
BANDS = 512
HORIZONS = 64


PI = 3.141592653589793
EPS = 1e-06
RING_MAX = 4


def encode(coords):
    freq = jnp.linspace(1.0, BANDS / 2.0, BANDS).astype(jnp.float32)
    angle = PI * freq[None, :, None] * coords[:, None, :]
    table = jnp.concatenate([jnp.sin(angle), jnp.cos(angle)], axis=0)
    return table.reshape(6 * BANDS, coords.shape[1]).T.astype(jnp.bfloat16)


def ring_gather(x, axis, n):
    if n == 1:
        return x
    if n > RING_MAX:
        return lax.all_gather(x, axis, axis=0, tiled=True)
    idx = lax.axis_index(axis)
    blocks = [x]
    for s in range(1, n):
        blocks.append(lax.ppermute(x, axis, [(i, (i - s) % n) for i in range(n)]))
    flipped = jnp.stack(blocks)
    ordered = jnp.roll(flipped, idx, axis=0)
    return ordered.reshape((n * x.shape[0],) + x.shape[1:])


def on_device(
    coords,
    horizon_ids,
    horizon_levels,
    latents,
    kv_weight,
    cross_out,
    norm_gains,
    self_qkv,
    self_out,
    dec_kv,
    dec_query,
    readout,
    *,
    n_picks,
    n_heads,
):
    high = lax.Precision.HIGHEST
    scale = HEAD ** (-0.5)
    count = coords.shape[1]
    width = latents.shape[1]
    lat_rows = latents.shape[0]
    local = kv_weight.shape[2]
    nheads = local // HEAD
    column = lax.axis_index("heads") * local
    enc = encode(coords)
    cross_full = ring_gather(cross_out, "heads", n_heads)
    piece = lax.all_gather(kv_weight, "picks", axis=0, tiled=True)
    cross_full, piece = lax.optimization_barrier((cross_full, piece))
    keys_vals = jnp.dot(
        enc, piece.reshape(piece.shape[0], 2 * local), preferred_element_type=jnp.float32
    ).astype(jnp.bfloat16)
    keys = keys_vals[:, :local].reshape(count, nheads, HEAD)
    values = keys_vals[:, local:].reshape(count, nheads, HEAD)
    queries = lax.dynamic_slice_in_dim(latents, column, local, 1).reshape(lat_rows, nheads, HEAD)
    scores = jnp.einsum("lhc,thc->hlt", queries, keys, preferred_element_type=jnp.float32) * scale
    top = jnp.max(scores, axis=2)
    expo = jnp.exp(scores - top[:, :, None])
    total = jnp.sum(expo, axis=2)
    numer = jnp.einsum(
        "hlt,thc->hlc", expo.astype(jnp.bfloat16), values, preferred_element_type=jnp.float32
    )
    all_numer = lax.all_gather(numer.astype(jnp.bfloat16), "picks", axis=0, tiled=False)
    all_stats = lax.all_gather(jnp.stack([top, total]), "picks", axis=0, tiled=False)
    best = jnp.max(all_stats[:, 0], axis=0)
    factor = jnp.exp(all_stats[:, 0] - best[None])
    merged_total = jnp.sum(factor * all_stats[:, 1], axis=0)
    merged_numer = jnp.einsum(
        "phl,phlc->hlc", factor, all_numer.astype(jnp.float32), precision=high
    )
    attended = (
        (merged_numer / merged_total[:, :, None])
        .transpose(1, 0, 2)
        .reshape(lat_rows, local)
        .astype(jnp.bfloat16)
    )
    dq_local, attended = lax.optimization_barrier((dec_query, attended))
    dq_full = lax.all_gather(dq_local, "picks", axis=0, tiled=True)
    gain_two = lax.dynamic_slice_in_dim(norm_gains[1], column, local, 0)
    attended_full = ring_gather(attended.T, "heads", n_heads).T
    whole = latents.astype(jnp.float32) + jnp.dot(
        attended_full, cross_full, preferred_element_type=jnp.float32
    )
    power = jnp.mean(whole * whole, axis=1, keepdims=True)
    normed = (whole * lax.rsqrt(power + EPS) * norm_gains[0][None, :]).astype(jnp.bfloat16)
    state = lax.dynamic_slice_in_dim(whole, column, local, 1)
    qkv = jnp.einsum("ld,kde->kle", normed, self_qkv, preferred_element_type=jnp.float32).astype(
        jnp.bfloat16
    )
    self_q = qkv[0].reshape(lat_rows, nheads, HEAD)
    self_k = qkv[1].reshape(lat_rows, nheads, HEAD)
    self_v = qkv[2].reshape(lat_rows, nheads, HEAD)
    inner = jnp.einsum("lhc,mhc->hlm", self_q, self_k, preferred_element_type=jnp.float32) * scale
    raised = jnp.exp(inner)
    probs = (raised / jnp.sum(raised, axis=2, keepdims=True)).astype(jnp.bfloat16)
    head_out = (
        jnp.einsum("hlm,mhc->lhc", probs, self_v, preferred_element_type=jnp.float32)
        .astype(jnp.bfloat16)
        .reshape(lat_rows, local)
    )
    every_head = ring_gather(head_out.T, "heads", n_heads).T
    latents_out = state + jnp.dot(every_head, self_out, preferred_element_type=jnp.float32)
    gained = (latents_out * gain_two[None, :]).astype(jnp.bfloat16)
    gained_full = ring_gather(gained.T, "heads", n_heads).T
    power_two = lax.psum(jnp.sum(latents_out * latents_out, axis=1), "heads")
    row_scale = lax.rsqrt(power_two / width + EPS)
    dec = (
        jnp.einsum("ld,kde->kle", gained_full, dec_kv, preferred_element_type=jnp.float32)
        * row_scale[None, :, None]
    ).astype(jnp.bfloat16)
    dec_keys = dec[0].reshape(lat_rows, nheads, HEAD)
    dec_vals = dec[1].reshape(lat_rows, nheads, HEAD)
    query = jnp.dot(enc, dq_full, preferred_element_type=jnp.float32).astype(jnp.bfloat16)
    dec_q = query.reshape(count, nheads, HEAD)
    logits = jnp.einsum("thc,lhc->htl", dec_q, dec_keys, preferred_element_type=jnp.float32) * scale
    lifted = jnp.exp(logits)
    weights = lifted / jnp.sum(lifted, axis=2, keepdims=True)
    out = jnp.einsum(
        "htl,lhc->thc", weights.astype(jnp.bfloat16), dec_vals, preferred_element_type=jnp.float32
    )
    read = readout.reshape(nheads, HEAD)
    field = lax.psum(jnp.sum(out * read[None, :, :], axis=(1, 2)), "heads")
    onehot = (horizon_ids[:, None] == jnp.arange(HORIZONS, dtype=jnp.int32)[None, :]).astype(
        jnp.float32
    )
    target = jnp.sum(onehot * horizon_levels[None, :], axis=1)
    miss = field - target
    value_read = jnp.einsum("lhc,hc->hl", dec_vals.astype(jnp.float32), read, precision=high)
    dprob = miss[None, :, None] * value_read[:, None, :]
    dscore = (weights * (dprob - jnp.sum(dprob * weights, axis=2, keepdims=True))).astype(
        jnp.bfloat16
    )
    dquery = (
        (jnp.einsum("htl,lhc->thc", dscore, dec_keys, preferred_element_type=jnp.float32) * scale)
        .reshape(count, local)
        .astype(jnp.bfloat16)
    )
    grad_query = lax.psum_scatter(
        jnp.dot(enc.T, dquery, preferred_element_type=jnp.float32).astype(jnp.bfloat16),
        "picks",
        scatter_dimension=0,
        tiled=True,
    ).astype(jnp.float32)
    return (field, latents_out, grad_query)


def solution(mesh):
    in_specs = (
        P(None, ("groups", "picks")),
        P(("groups", "picks")),
        P("groups"),
        P(),
        P("picks", None, "heads"),
        P("heads", None),
        P(),
        P(None, None, "heads"),
        P(None, "heads"),
        P(None, None, "heads"),
        P("picks", "heads"),
        P("heads"),
    )
    out_specs = (P(("groups", "picks")), P("groups", "heads"), P(("groups", "picks"), "heads"))
    body = functools.partial(
        on_device, n_picks=mesh.shape["picks"], n_heads=mesh.shape["heads"]
    )
    return jax.shard_map(body, mesh=mesh, in_specs=in_specs, out_specs=out_specs, check_vma=False)
```

```python
import functools

import jax
import jax.numpy as jnp
from jax import lax
from jax.sharding import PartitionSpec as P

HEAD = 128
BANDS = 512
HORIZONS = 64


PI = 3.141592653589793
EPS = 1e-06
RING_MAX = 4


def encode(coords):
    freq = jnp.linspace(1.0, BANDS / 2.0, BANDS).astype(jnp.float32)
    angle = PI * freq[None, :, None] * coords[:, None, :]
    table = jnp.concatenate([jnp.sin(angle), jnp.cos(angle)], axis=0)
    return table.reshape(6 * BANDS, coords.shape[1]).T.astype(jnp.bfloat16)


def ring_gather(x, axis, n):
    if n == 1:
        return x
    if n > RING_MAX:
        return lax.all_gather(x, axis, axis=0, tiled=True)
    idx = lax.axis_index(axis)
    blocks = [x]
    for s in range(1, n):
        blocks.append(lax.ppermute(x, axis, [(i, (i - s) % n) for i in range(n)]))
    flipped = jnp.stack(blocks)
    ordered = jnp.roll(flipped, idx, axis=0)
    return ordered.reshape((n * x.shape[0],) + x.shape[1:])


def fetch_rows(kv_weight, n_picks, n_groups):
    if n_groups != 2:
        return lax.all_gather(kv_weight, "picks", axis=0, tiled=True)
    g = lax.axis_index("groups")
    rows = kv_weight.shape[0] // 2
    mine = lax.dynamic_slice_in_dim(kv_weight, g * rows, rows, 0)
    first = max(8, (2 * rows // 3) // 8 * 8)
    bounds = [(0, first), (first, rows)] if first < rows else [(0, rows)]
    own, other = [], []
    for lo, hi in bounds:
        gathered = lax.all_gather(mine[lo:hi], "picks", axis=0, tiled=False)
        own.append(gathered)
        other.append(lax.ppermute(gathered, "groups", [(0, 1), (1, 0)]))
    halves = jnp.stack([jnp.concatenate(own, axis=1), jnp.concatenate(other, axis=1)], axis=1)
    halves = jnp.roll(halves, g, axis=1)
    return halves.reshape((n_picks * kv_weight.shape[0],) + kv_weight.shape[1:])


def on_device(
    coords,
    horizon_ids,
    horizon_levels,
    latents,
    kv_weight,
    cross_out,
    norm_gains,
    self_qkv,
    self_out,
    dec_kv,
    dec_query,
    readout,
    *,
    n_picks,
    n_heads,
    n_groups,
):
    high = lax.Precision.HIGHEST
    scale = HEAD ** (-0.5)
    count = coords.shape[1]
    width = latents.shape[1]
    lat_rows = latents.shape[0]
    local = kv_weight.shape[2]
    nheads = local // HEAD
    column = lax.axis_index("heads") * local
    enc = encode(coords)
    cross_full = ring_gather(cross_out, "heads", n_heads)
    piece = fetch_rows(kv_weight, n_picks, n_groups)
    cross_full, piece = lax.optimization_barrier((cross_full, piece))
    keys_vals = jnp.dot(
        enc, piece.reshape(piece.shape[0], 2 * local), preferred_element_type=jnp.float32
    ).astype(jnp.bfloat16)
    keys = keys_vals[:, :local].reshape(count, nheads, HEAD)
    values = keys_vals[:, local:].reshape(count, nheads, HEAD)
    queries = lax.dynamic_slice_in_dim(latents, column, local, 1).reshape(lat_rows, nheads, HEAD)
    scores = jnp.einsum("lhc,thc->hlt", queries, keys, preferred_element_type=jnp.float32) * scale
    top = jnp.max(scores, axis=2)
    expo = jnp.exp(scores - top[:, :, None])
    total = jnp.sum(expo, axis=2)
    numer = jnp.einsum(
        "hlt,thc->hlc", expo.astype(jnp.bfloat16), values, preferred_element_type=jnp.float32
    )
    all_numer = lax.all_gather(numer.astype(jnp.bfloat16), "picks", axis=0, tiled=False)
    all_stats = lax.all_gather(jnp.stack([top, total]), "picks", axis=0, tiled=False)
    best = jnp.max(all_stats[:, 0], axis=0)
    factor = jnp.exp(all_stats[:, 0] - best[None])
    merged_total = jnp.sum(factor * all_stats[:, 1], axis=0)
    merged_numer = jnp.einsum(
        "phl,phlc->hlc", factor, all_numer.astype(jnp.float32), precision=high
    )
    attended = (
        (merged_numer / merged_total[:, :, None])
        .transpose(1, 0, 2)
        .reshape(lat_rows, local)
        .astype(jnp.bfloat16)
    )
    out_full = ring_gather(self_out.T, "heads", n_heads).T
    out_full, attended = lax.optimization_barrier((out_full, attended))
    dq_local, attended = lax.optimization_barrier((dec_query, attended))
    dq_full = lax.all_gather(dq_local, "picks", axis=0, tiled=True)
    attended_full = ring_gather(attended.T, "heads", n_heads).T
    whole = latents.astype(jnp.float32) + jnp.dot(
        attended_full, cross_full, preferred_element_type=jnp.float32
    )
    power = jnp.mean(whole * whole, axis=1, keepdims=True)
    normed = (whole * lax.rsqrt(power + EPS) * norm_gains[0][None, :]).astype(jnp.bfloat16)
    state = lax.dynamic_slice_in_dim(whole, column, local, 1)
    qkv = jnp.einsum("ld,kde->kle", normed, self_qkv, preferred_element_type=jnp.float32).astype(
        jnp.bfloat16
    )
    self_q = qkv[0].reshape(lat_rows, nheads, HEAD)
    self_k = qkv[1].reshape(lat_rows, nheads, HEAD)
    self_v = qkv[2].reshape(lat_rows, nheads, HEAD)
    inner = jnp.einsum("lhc,mhc->hlm", self_q, self_k, preferred_element_type=jnp.float32) * scale
    raised = jnp.exp(inner)
    probs = (raised / jnp.sum(raised, axis=2, keepdims=True)).astype(jnp.bfloat16)
    head_out = (
        jnp.einsum("hlm,mhc->lhc", probs, self_v, preferred_element_type=jnp.float32)
        .astype(jnp.bfloat16)
        .reshape(lat_rows, local)
    )
    every_head = ring_gather(head_out.T, "heads", n_heads).T
    out_whole = whole + jnp.dot(every_head, out_full, preferred_element_type=jnp.float32)
    latents_out = lax.dynamic_slice_in_dim(out_whole, column, local, 1)
    power_two = jnp.mean(out_whole * out_whole, axis=1, keepdims=True)
    normed2 = (out_whole * lax.rsqrt(power_two + EPS) * norm_gains[1][None, :]).astype(
        jnp.bfloat16
    )
    dec = jnp.einsum("ld,kde->kle", normed2, dec_kv, preferred_element_type=jnp.float32).astype(
        jnp.bfloat16
    )
    dec_keys = dec[0].reshape(lat_rows, nheads, HEAD)
    dec_vals = dec[1].reshape(lat_rows, nheads, HEAD)
    query = jnp.dot(enc, dq_full, preferred_element_type=jnp.float32).astype(jnp.bfloat16)
    dec_q = query.reshape(count, nheads, HEAD)
    logits = jnp.einsum("thc,lhc->htl", dec_q, dec_keys, preferred_element_type=jnp.float32) * scale
    lifted = jnp.exp(logits)
    weights = lifted / jnp.sum(lifted, axis=2, keepdims=True)
    out = jnp.einsum(
        "htl,lhc->thc", weights.astype(jnp.bfloat16), dec_vals, preferred_element_type=jnp.float32
    )
    read = readout.reshape(nheads, HEAD)
    field = lax.psum(jnp.sum(out * read[None, :, :], axis=(1, 2)), "heads")
    onehot = (horizon_ids[:, None] == jnp.arange(HORIZONS, dtype=jnp.int32)[None, :]).astype(
        jnp.float32
    )
    target = jnp.sum(onehot * horizon_levels[None, :], axis=1)
    miss = field - target
    value_read = jnp.einsum("lhc,hc->hl", dec_vals.astype(jnp.float32), read, precision=high)
    dprob = miss[None, :, None] * value_read[:, None, :]
    dscore = (weights * (dprob - jnp.sum(dprob * weights, axis=2, keepdims=True))).astype(
        jnp.bfloat16
    )
    dquery = (
        (jnp.einsum("htl,lhc->thc", dscore, dec_keys, preferred_element_type=jnp.float32) * scale)
        .reshape(count, local)
        .astype(jnp.bfloat16)
    )
    grad_query = lax.psum_scatter(
        jnp.dot(enc.T, dquery, preferred_element_type=jnp.float32).astype(jnp.bfloat16),
        "picks",
        scatter_dimension=0,
        tiled=True,
    ).astype(jnp.float32)
    return (field, latents_out, grad_query)


def solution(mesh):
    in_specs = (
        P(None, ("groups", "picks")),
        P(("groups", "picks")),
        P("groups"),
        P(),
        P("picks", None, "heads"),
        P("heads", None),
        P(),
        P(None, None, "heads"),
        P(None, "heads"),
        P(None, None, "heads"),
        P("picks", "heads"),
        P("heads"),
    )
    out_specs = (P(("groups", "picks")), P("groups", "heads"), P(("groups", "picks"), "heads"))
    body = functools.partial(
        on_device,
        n_picks=mesh.shape["picks"],
        n_heads=mesh.shape["heads"],
        n_groups=mesh.shape["groups"],
    )
    return jax.shard_map(body, mesh=mesh, in_specs=in_specs, out_specs=out_specs, check_vma=False)
```

```python
import functools

import jax
import jax.numpy as jnp
from jax import lax
from jax.sharding import PartitionSpec as P

HEAD = 128
BANDS = 512
HORIZONS = 64


PI = 3.141592653589793
EPS = 1e-06
RING_MAX = 4


def encode(coords):
    freq = jnp.linspace(1.0, BANDS / 2.0, BANDS).astype(jnp.float32)
    angle = PI * freq[None, :, None] * coords[:, None, :]
    table = jnp.concatenate([jnp.sin(angle), jnp.cos(angle)], axis=0)
    return table.reshape(6 * BANDS, coords.shape[1]).T.astype(jnp.bfloat16)


def ring_gather(x, axis, n):
    if n == 1:
        return x
    if n > RING_MAX:
        return lax.all_gather(x, axis, axis=0, tiled=True)
    idx = lax.axis_index(axis)
    blocks = [x]
    for s in range(1, n):
        blocks.append(lax.ppermute(x, axis, [(i, (i - s) % n) for i in range(n)]))
    flipped = jnp.stack(blocks)
    ordered = jnp.roll(flipped, idx, axis=0)
    return ordered.reshape((n * x.shape[0],) + x.shape[1:])


def fetch_rows(kv_weight, n_picks, n_groups):
    if n_groups != 2:
        return lax.all_gather(kv_weight, "picks", axis=0, tiled=True)
    g = lax.axis_index("groups")
    rows = kv_weight.shape[0] // 2
    mine = lax.dynamic_slice_in_dim(kv_weight, g * rows, rows, 0)
    first = max(8, (2 * rows // 3) // 8 * 8)
    bounds = [(0, first), (first, rows)] if first < rows else [(0, rows)]
    own, other = [], []
    for lo, hi in bounds:
        gathered = lax.all_gather(mine[lo:hi], "picks", axis=0, tiled=False)
        own.append(gathered)
        other.append(lax.ppermute(gathered, "groups", [(0, 1), (1, 0)]))
    halves = jnp.stack([jnp.concatenate(own, axis=1), jnp.concatenate(other, axis=1)], axis=1)
    halves = jnp.roll(halves, g, axis=1)
    return halves.reshape((n_picks * kv_weight.shape[0],) + kv_weight.shape[1:])


def on_device(
    coords,
    horizon_ids,
    horizon_levels,
    latents,
    kv_weight,
    cross_out,
    norm_gains,
    self_qkv,
    self_out,
    dec_kv,
    dec_query,
    readout,
    *,
    n_picks,
    n_heads,
    n_groups,
):
    high = lax.Precision.HIGHEST
    scale = HEAD ** (-0.5)
    count = coords.shape[1]
    width = latents.shape[1]
    lat_rows = latents.shape[0]
    local = kv_weight.shape[2]
    nheads = local // HEAD
    column = lax.axis_index("heads") * local
    enc = encode(coords)
    cross_full = ring_gather(cross_out, "heads", n_heads)
    piece = lax.all_gather(kv_weight, "picks", axis=0, tiled=True)
    cross_full, piece = lax.optimization_barrier((cross_full, piece))
    keys_vals = jnp.dot(
        enc, piece.reshape(piece.shape[0], 2 * local), preferred_element_type=jnp.float32
    ).astype(jnp.bfloat16)
    keys = keys_vals[:, :local].reshape(count, nheads, HEAD)
    values = keys_vals[:, local:].reshape(count, nheads, HEAD)
    queries = lax.dynamic_slice_in_dim(latents, column, local, 1).reshape(lat_rows, nheads, HEAD)
    scores = jnp.einsum("lhc,thc->hlt", queries, keys, preferred_element_type=jnp.float32) * scale
    top = jnp.max(scores, axis=2)
    expo = jnp.exp(scores - top[:, :, None])
    total = jnp.sum(expo, axis=2)
    numer = jnp.einsum(
        "hlt,thc->hlc", expo.astype(jnp.bfloat16), values, preferred_element_type=jnp.float32
    )
    all_numer = lax.all_gather(numer.astype(jnp.bfloat16), "picks", axis=0, tiled=False)
    all_stats = lax.all_gather(jnp.stack([top, total]), "picks", axis=0, tiled=False)
    best = jnp.max(all_stats[:, 0], axis=0)
    factor = jnp.exp(all_stats[:, 0] - best[None])
    merged_total = jnp.sum(factor * all_stats[:, 1], axis=0)
    merged_numer = jnp.einsum(
        "phl,phlc->hlc", factor, all_numer.astype(jnp.float32), precision=high
    )
    attended = (
        (merged_numer / merged_total[:, :, None])
        .transpose(1, 0, 2)
        .reshape(lat_rows, local)
        .astype(jnp.bfloat16)
    )
    out_full = ring_gather(self_out.T, "heads", n_heads).T
    out_full, attended = lax.optimization_barrier((out_full, attended))
    dq_local, attended = lax.optimization_barrier((dec_query, attended))
    dq_full = lax.all_gather(dq_local, "picks", axis=0, tiled=True)
    attended_full = ring_gather(attended.T, "heads", n_heads).T
    whole = latents.astype(jnp.float32) + jnp.dot(
        attended_full, cross_full, preferred_element_type=jnp.float32
    )
    power = jnp.mean(whole * whole, axis=1, keepdims=True)
    normed = (whole * lax.rsqrt(power + EPS) * norm_gains[0][None, :]).astype(jnp.bfloat16)
    state = lax.dynamic_slice_in_dim(whole, column, local, 1)
    qkv = jnp.einsum("ld,kde->kle", normed, self_qkv, preferred_element_type=jnp.float32).astype(
        jnp.bfloat16
    )
    self_q = qkv[0].reshape(lat_rows, nheads, HEAD)
    self_k = qkv[1].reshape(lat_rows, nheads, HEAD)
    self_v = qkv[2].reshape(lat_rows, nheads, HEAD)
    inner = jnp.einsum("lhc,mhc->hlm", self_q, self_k, preferred_element_type=jnp.float32) * scale
    raised = jnp.exp(inner)
    probs = (raised / jnp.sum(raised, axis=2, keepdims=True)).astype(jnp.bfloat16)
    head_out = (
        jnp.einsum("hlm,mhc->lhc", probs, self_v, preferred_element_type=jnp.float32)
        .astype(jnp.bfloat16)
        .reshape(lat_rows, local)
    )
    every_head = ring_gather(head_out.T, "heads", n_heads).T
    out_whole = whole + jnp.dot(every_head, out_full, preferred_element_type=jnp.float32)
    latents_out = lax.dynamic_slice_in_dim(out_whole, column, local, 1)
    power_two = jnp.mean(out_whole * out_whole, axis=1, keepdims=True)
    normed2 = (out_whole * lax.rsqrt(power_two + EPS) * norm_gains[1][None, :]).astype(
        jnp.bfloat16
    )
    dec = jnp.einsum("ld,kde->kle", normed2, dec_kv, preferred_element_type=jnp.float32).astype(
        jnp.bfloat16
    )
    dec_keys = dec[0].reshape(lat_rows, nheads, HEAD)
    dec_vals = dec[1].reshape(lat_rows, nheads, HEAD)
    query = jnp.dot(enc, dq_full, preferred_element_type=jnp.float32).astype(jnp.bfloat16)
    dec_q = query.reshape(count, nheads, HEAD)
    logits = jnp.einsum("thc,lhc->htl", dec_q, dec_keys, preferred_element_type=jnp.float32) * scale
    lifted = jnp.exp(logits)
    weights = lifted / jnp.sum(lifted, axis=2, keepdims=True)
    out = jnp.einsum(
        "htl,lhc->thc", weights.astype(jnp.bfloat16), dec_vals, preferred_element_type=jnp.float32
    )
    read = readout.reshape(nheads, HEAD)
    field = lax.psum(jnp.sum(out * read[None, :, :], axis=(1, 2)), "heads")
    onehot = (horizon_ids[:, None] == jnp.arange(HORIZONS, dtype=jnp.int32)[None, :]).astype(
        jnp.float32
    )
    target = jnp.sum(onehot * horizon_levels[None, :], axis=1)
    miss = field - target
    value_read = jnp.einsum("lhc,hc->hl", dec_vals.astype(jnp.float32), read, precision=high)
    dprob = miss[None, :, None] * value_read[:, None, :]
    dscore = (weights * (dprob - jnp.sum(dprob * weights, axis=2, keepdims=True))).astype(
        jnp.bfloat16
    )
    dquery = (
        (jnp.einsum("htl,lhc->thc", dscore, dec_keys, preferred_element_type=jnp.float32) * scale)
        .reshape(count, local)
        .astype(jnp.bfloat16)
    )
    grad_query = lax.psum_scatter(
        jnp.dot(enc.T, dquery, preferred_element_type=jnp.float32).astype(jnp.bfloat16),
        "picks",
        scatter_dimension=0,
        tiled=True,
    ).astype(jnp.float32)
    return (field, latents_out, grad_query)


def solution(mesh):
    in_specs = (
        P(None, ("groups", "picks")),
        P(("groups", "picks")),
        P("groups"),
        P(),
        P("picks", None, "heads"),
        P("heads", None),
        P(),
        P(None, None, "heads"),
        P(None, "heads"),
        P(None, None, "heads"),
        P("picks", "heads"),
        P("heads"),
    )
    out_specs = (P(("groups", "picks")), P("groups", "heads"), P(("groups", "picks"), "heads"))
    body = functools.partial(
        on_device,
        n_picks=mesh.shape["picks"],
        n_heads=mesh.shape["heads"],
        n_groups=mesh.shape["groups"],
    )
    return jax.shard_map(body, mesh=mesh, in_specs=in_specs, out_specs=out_specs, check_vma=False)
```

```python
import functools

import jax
import jax.numpy as jnp
from jax import lax
from jax.sharding import PartitionSpec as P

HEAD = 128
BANDS = 512
HORIZONS = 64


PI = 3.141592653589793
EPS = 1e-06
RING_MAX = 4


def encode(coords):
    freq = jnp.linspace(1.0, BANDS / 2.0, BANDS).astype(jnp.float32)
    angle = PI * freq[None, :, None] * coords[:, None, :]
    table = jnp.concatenate([jnp.sin(angle), jnp.cos(angle)], axis=0)
    return table.reshape(6 * BANDS, coords.shape[1]).T.astype(jnp.bfloat16)


def ring_gather(x, axis, n):
    if n == 1:
        return x
    if n > RING_MAX:
        return lax.all_gather(x, axis, axis=0, tiled=True)
    idx = lax.axis_index(axis)
    blocks = [x]
    for s in range(1, n):
        blocks.append(lax.ppermute(x, axis, [(i, (i - s) % n) for i in range(n)]))
    flipped = jnp.stack(blocks)
    ordered = jnp.roll(flipped, idx, axis=0)
    return ordered.reshape((n * x.shape[0],) + x.shape[1:])


def fetch_rows(kv_weight, n_picks, n_groups):
    if n_groups != 2:
        return lax.all_gather(kv_weight, "picks", axis=0, tiled=True)
    g = lax.axis_index("groups")
    rows = kv_weight.shape[0] // 2
    mine = lax.dynamic_slice_in_dim(kv_weight, g * rows, rows, 0)
    first = max(8, (2 * rows // 3) // 8 * 8)
    bounds = [(0, first), (first, rows)] if first < rows else [(0, rows)]
    own, other = [], []
    for lo, hi in bounds:
        gathered = lax.all_gather(mine[lo:hi], "picks", axis=0, tiled=False)
        own.append(gathered)
        other.append(lax.ppermute(gathered, "groups", [(0, 1), (1, 0)]))
    halves = jnp.stack([jnp.concatenate(own, axis=1), jnp.concatenate(other, axis=1)], axis=1)
    halves = jnp.roll(halves, g, axis=1)
    return halves.reshape((n_picks * kv_weight.shape[0],) + kv_weight.shape[1:])


def pair_gather(x, axis, n):
    if n != 4:
        return ring_gather(x, axis, n)
    idx = lax.axis_index(axis)
    near = lax.ppermute(x, axis, [(k, k ^ 1) for k in range(n)])
    far = lax.ppermute(x, axis, [(k, k ^ 2) for k in range(n)])
    far_near = lax.ppermute(far, axis, [(k, k ^ 1) for k in range(n)])
    cand = jnp.stack([x, near, far, far_near])
    cand = jnp.where(idx % 2 == 1, cand[jnp.array([1, 0, 3, 2])], cand)
    cand = jnp.where(idx // 2 % 2 == 1, cand[jnp.array([2, 3, 0, 1])], cand)
    return cand.reshape((n * x.shape[0],) + x.shape[1:])


def on_device(
    coords,
    horizon_ids,
    horizon_levels,
    latents,
    kv_weight,
    cross_out,
    norm_gains,
    self_qkv,
    self_out,
    dec_kv,
    dec_query,
    readout,
    *,
    n_picks,
    n_heads,
    n_groups,
):
    high = lax.Precision.HIGHEST
    scale = HEAD ** (-0.5)
    count = coords.shape[1]
    width = latents.shape[1]
    lat_rows = latents.shape[0]
    local = kv_weight.shape[2]
    nheads = local // HEAD
    column = lax.axis_index("heads") * local
    enc = encode(coords)
    cross_full = pair_gather(cross_out, "heads", n_heads)
    piece = lax.all_gather(kv_weight, "picks", axis=0, tiled=True)
    cross_full, piece = lax.optimization_barrier((cross_full, piece))
    keys_vals = jnp.dot(
        enc, piece.reshape(piece.shape[0], 2 * local), preferred_element_type=jnp.float32
    ).astype(jnp.bfloat16)
    keys = keys_vals[:, :local].reshape(count, nheads, HEAD)
    values = keys_vals[:, local:].reshape(count, nheads, HEAD)
    queries = lax.dynamic_slice_in_dim(latents, column, local, 1).reshape(lat_rows, nheads, HEAD)
    scores = jnp.einsum("lhc,thc->hlt", queries, keys, preferred_element_type=jnp.float32) * scale
    top = jnp.max(scores, axis=2)
    expo = jnp.exp(scores - top[:, :, None])
    total = jnp.sum(expo, axis=2)
    numer = jnp.einsum(
        "hlt,thc->hlc", expo.astype(jnp.bfloat16), values, preferred_element_type=jnp.float32
    )
    all_numer = lax.all_gather(numer.astype(jnp.bfloat16), "picks", axis=0, tiled=False)
    all_stats = lax.all_gather(jnp.stack([top, total]), "picks", axis=0, tiled=False)
    best = jnp.max(all_stats[:, 0], axis=0)
    factor = jnp.exp(all_stats[:, 0] - best[None])
    merged_total = jnp.sum(factor * all_stats[:, 1], axis=0)
    merged_numer = jnp.einsum(
        "phl,phlc->hlc", factor, all_numer.astype(jnp.float32), precision=high
    )
    attended = (
        (merged_numer / merged_total[:, :, None])
        .transpose(1, 0, 2)
        .reshape(lat_rows, local)
        .astype(jnp.bfloat16)
    )
    out_full = pair_gather(self_out.T, "heads", n_heads).T
    out_full, attended = lax.optimization_barrier((out_full, attended))
    dq_local, attended = lax.optimization_barrier((dec_query, attended))
    dq_full = lax.all_gather(dq_local, "picks", axis=0, tiled=True)
    attended_full = pair_gather(attended.T, "heads", n_heads).T
    whole = latents.astype(jnp.float32) + jnp.dot(
        attended_full, cross_full, preferred_element_type=jnp.float32
    )
    power = jnp.mean(whole * whole, axis=1, keepdims=True)
    normed = (whole * lax.rsqrt(power + EPS) * norm_gains[0][None, :]).astype(jnp.bfloat16)
    state = lax.dynamic_slice_in_dim(whole, column, local, 1)
    qkv = jnp.einsum("ld,kde->kle", normed, self_qkv, preferred_element_type=jnp.float32).astype(
        jnp.bfloat16
    )
    self_q = qkv[0].reshape(lat_rows, nheads, HEAD)
    self_k = qkv[1].reshape(lat_rows, nheads, HEAD)
    self_v = qkv[2].reshape(lat_rows, nheads, HEAD)
    inner = jnp.einsum("lhc,mhc->hlm", self_q, self_k, preferred_element_type=jnp.float32) * scale
    raised = jnp.exp(inner)
    probs = (raised / jnp.sum(raised, axis=2, keepdims=True)).astype(jnp.bfloat16)
    head_out = (
        jnp.einsum("hlm,mhc->lhc", probs, self_v, preferred_element_type=jnp.float32)
        .astype(jnp.bfloat16)
        .reshape(lat_rows, local)
    )
    every_head = pair_gather(head_out.T, "heads", n_heads).T
    out_whole = whole + jnp.dot(every_head, out_full, preferred_element_type=jnp.float32)
    latents_out = lax.dynamic_slice_in_dim(out_whole, column, local, 1)
    power_two = jnp.mean(out_whole * out_whole, axis=1, keepdims=True)
    normed2 = (out_whole * lax.rsqrt(power_two + EPS) * norm_gains[1][None, :]).astype(
        jnp.bfloat16
    )
    dec = jnp.einsum("ld,kde->kle", normed2, dec_kv, preferred_element_type=jnp.float32).astype(
        jnp.bfloat16
    )
    dec_keys = dec[0].reshape(lat_rows, nheads, HEAD)
    dec_vals = dec[1].reshape(lat_rows, nheads, HEAD)
    query = jnp.dot(enc, dq_full, preferred_element_type=jnp.float32).astype(jnp.bfloat16)
    dec_q = query.reshape(count, nheads, HEAD)
    logits = jnp.einsum("thc,lhc->htl", dec_q, dec_keys, preferred_element_type=jnp.float32) * scale
    lifted = jnp.exp(logits)
    weights = lifted / jnp.sum(lifted, axis=2, keepdims=True)
    out = jnp.einsum(
        "htl,lhc->thc", weights.astype(jnp.bfloat16), dec_vals, preferred_element_type=jnp.float32
    )
    read = readout.reshape(nheads, HEAD)
    field = lax.psum(jnp.sum(out * read[None, :, :], axis=(1, 2)), "heads")
    onehot = (horizon_ids[:, None] == jnp.arange(HORIZONS, dtype=jnp.int32)[None, :]).astype(
        jnp.float32
    )
    target = jnp.sum(onehot * horizon_levels[None, :], axis=1)
    miss = field - target
    value_read = jnp.einsum("lhc,hc->hl", dec_vals.astype(jnp.float32), read, precision=high)
    dprob = miss[None, :, None] * value_read[:, None, :]
    dscore = (weights * (dprob - jnp.sum(dprob * weights, axis=2, keepdims=True))).astype(
        jnp.bfloat16
    )
    dquery = (
        (jnp.einsum("htl,lhc->thc", dscore, dec_keys, preferred_element_type=jnp.float32) * scale)
        .reshape(count, local)
        .astype(jnp.bfloat16)
    )
    grad_query = lax.psum_scatter(
        jnp.dot(enc.T, dquery, preferred_element_type=jnp.float32).astype(jnp.bfloat16),
        "picks",
        scatter_dimension=0,
        tiled=True,
    ).astype(jnp.float32)
    return (field, latents_out, grad_query)


def solution(mesh):
    in_specs = (
        P(None, ("groups", "picks")),
        P(("groups", "picks")),
        P("groups"),
        P(),
        P("picks", None, "heads"),
        P("heads", None),
        P(),
        P(None, None, "heads"),
        P(None, "heads"),
        P(None, None, "heads"),
        P("picks", "heads"),
        P("heads"),
    )
    out_specs = (P(("groups", "picks")), P("groups", "heads"), P(("groups", "picks"), "heads"))
    body = functools.partial(
        on_device,
        n_picks=mesh.shape["picks"],
        n_heads=mesh.shape["heads"],
        n_groups=mesh.shape["groups"],
    )
    return jax.shard_map(body, mesh=mesh, in_specs=in_specs, out_specs=out_specs, check_vma=False)
```

```python
import functools

import jax
import jax.numpy as jnp
from jax import lax
from jax.sharding import PartitionSpec as P

HEAD = 128
BANDS = 512
HORIZONS = 64


PI = 3.141592653589793
EPS = 1e-06
RING_MAX = 4


def encode(coords):
    freq = jnp.linspace(1.0, BANDS / 2.0, BANDS).astype(jnp.float32)
    angle = PI * freq[None, :, None] * coords[:, None, :]
    table = jnp.concatenate([jnp.sin(angle), jnp.cos(angle)], axis=0)
    return table.reshape(6 * BANDS, coords.shape[1]).T.astype(jnp.bfloat16)


def ring_gather(x, axis, n):
    if n == 1:
        return x
    if n > RING_MAX:
        return lax.all_gather(x, axis, axis=0, tiled=True)
    idx = lax.axis_index(axis)
    blocks = [x]
    for s in range(1, n):
        blocks.append(lax.ppermute(x, axis, [(i, (i - s) % n) for i in range(n)]))
    flipped = jnp.stack(blocks)
    ordered = jnp.roll(flipped, idx, axis=0)
    return ordered.reshape((n * x.shape[0],) + x.shape[1:])


def fetch_rows(kv_weight, n_picks, n_groups):
    if n_groups != 2:
        return lax.all_gather(kv_weight, "picks", axis=0, tiled=True)
    g = lax.axis_index("groups")
    rows = kv_weight.shape[0] // 2
    mine = lax.dynamic_slice_in_dim(kv_weight, g * rows, rows, 0)
    first = max(8, (2 * rows // 3) // 8 * 8)
    bounds = [(0, first), (first, rows)] if first < rows else [(0, rows)]
    own, other = [], []
    for lo, hi in bounds:
        gathered = lax.all_gather(mine[lo:hi], "picks", axis=0, tiled=False)
        own.append(gathered)
        other.append(lax.ppermute(gathered, "groups", [(0, 1), (1, 0)]))
    halves = jnp.stack([jnp.concatenate(own, axis=1), jnp.concatenate(other, axis=1)], axis=1)
    halves = jnp.roll(halves, g, axis=1)
    return halves.reshape((n_picks * kv_weight.shape[0],) + kv_weight.shape[1:])


def pair_sum(x, axis, n):
    if n != 4:
        return lax.psum(x, axis)
    x = x + lax.ppermute(x, axis, [(k, k ^ 1) for k in range(n)])
    return x + lax.ppermute(x, axis, [(k, k ^ 2) for k in range(n)])


def on_device(
    coords,
    horizon_ids,
    horizon_levels,
    latents,
    kv_weight,
    cross_out,
    norm_gains,
    self_qkv,
    self_out,
    dec_kv,
    dec_query,
    readout,
    *,
    n_picks,
    n_heads,
    n_groups,
):
    high = lax.Precision.HIGHEST
    scale = HEAD ** (-0.5)
    count = coords.shape[1]
    width = latents.shape[1]
    lat_rows = latents.shape[0]
    local = kv_weight.shape[2]
    nheads = local // HEAD
    column = lax.axis_index("heads") * local
    enc = encode(coords)
    cross_full = ring_gather(cross_out, "heads", n_heads)
    piece = lax.all_gather(
        kv_weight.reshape(kv_weight.shape[0], 2 * local), "picks", axis=0, tiled=True
    )
    cross_full, piece = lax.optimization_barrier((cross_full, piece))
    keys_vals = jnp.dot(
        enc, piece.reshape(piece.shape[0], 2 * local), preferred_element_type=jnp.float32
    ).astype(jnp.bfloat16)
    keys = keys_vals[:, :local].reshape(count, nheads, HEAD)
    values = keys_vals[:, local:].reshape(count, nheads, HEAD)
    queries = lax.dynamic_slice_in_dim(latents, column, local, 1).reshape(lat_rows, nheads, HEAD)
    scores = jnp.einsum("lhc,thc->hlt", queries, keys, preferred_element_type=jnp.float32) * scale
    top = jnp.max(scores, axis=2)
    expo = jnp.exp(scores - top[:, :, None])
    total = jnp.sum(expo, axis=2)
    numer = jnp.einsum(
        "hlt,thc->hlc", expo.astype(jnp.bfloat16), values, preferred_element_type=jnp.float32
    )
    all_numer = lax.all_gather(numer.astype(jnp.bfloat16), "picks", axis=0, tiled=False)
    all_stats = lax.all_gather(jnp.stack([top, total]), "picks", axis=0, tiled=False)
    best = jnp.max(all_stats[:, 0], axis=0)
    factor = jnp.exp(all_stats[:, 0] - best[None])
    merged_total = jnp.sum(factor * all_stats[:, 1], axis=0)
    merged_numer = jnp.einsum(
        "phl,phlc->hlc", factor, all_numer.astype(jnp.float32), precision=high
    )
    attended = (
        (merged_numer / merged_total[:, :, None])
        .transpose(1, 0, 2)
        .reshape(lat_rows, local)
        .astype(jnp.bfloat16)
    )
    out_full = ring_gather(self_out.T, "heads", n_heads).T
    out_full, attended = lax.optimization_barrier((out_full, attended))
    dq_local, attended = lax.optimization_barrier((dec_query, attended))
    dq_full = lax.all_gather(dq_local, "picks", axis=0, tiled=True)
    attended_full = ring_gather(attended.T, "heads", n_heads).T
    whole = latents.astype(jnp.float32) + jnp.dot(
        attended_full, cross_full, preferred_element_type=jnp.float32
    )
    power = jnp.mean(whole * whole, axis=1, keepdims=True)
    normed = (whole * lax.rsqrt(power + EPS) * norm_gains[0][None, :]).astype(jnp.bfloat16)
    state = lax.dynamic_slice_in_dim(whole, column, local, 1)
    qkv = jnp.einsum("ld,kde->kle", normed, self_qkv, preferred_element_type=jnp.float32).astype(
        jnp.bfloat16
    )
    self_q = qkv[0].reshape(lat_rows, nheads, HEAD)
    self_k = qkv[1].reshape(lat_rows, nheads, HEAD)
    self_v = qkv[2].reshape(lat_rows, nheads, HEAD)
    inner = jnp.einsum("lhc,mhc->hlm", self_q, self_k, preferred_element_type=jnp.float32) * scale
    raised = jnp.exp(inner)
    probs = (raised / jnp.sum(raised, axis=2, keepdims=True)).astype(jnp.bfloat16)
    head_out = (
        jnp.einsum("hlm,mhc->lhc", probs, self_v, preferred_element_type=jnp.float32)
        .astype(jnp.bfloat16)
        .reshape(lat_rows, local)
    )
    every_head = ring_gather(head_out.T, "heads", n_heads).T
    out_whole = whole + jnp.dot(every_head, out_full, preferred_element_type=jnp.float32)
    latents_out = lax.dynamic_slice_in_dim(out_whole, column, local, 1)
    power_two = jnp.mean(out_whole * out_whole, axis=1, keepdims=True)
    normed2 = (out_whole * lax.rsqrt(power_two + EPS) * norm_gains[1][None, :]).astype(
        jnp.bfloat16
    )
    dec = jnp.einsum("ld,kde->kle", normed2, dec_kv, preferred_element_type=jnp.float32).astype(
        jnp.bfloat16
    )
    dec_keys = dec[0].reshape(lat_rows, nheads, HEAD)
    dec_vals = dec[1].reshape(lat_rows, nheads, HEAD)
    query = jnp.dot(enc, dq_full, preferred_element_type=jnp.float32).astype(jnp.bfloat16)
    dec_q = query.reshape(count, nheads, HEAD)
    logits = jnp.einsum("thc,lhc->htl", dec_q, dec_keys, preferred_element_type=jnp.float32) * scale
    lifted = jnp.exp(logits)
    weights = lifted / jnp.sum(lifted, axis=2, keepdims=True)
    out = jnp.einsum(
        "htl,lhc->thc", weights.astype(jnp.bfloat16), dec_vals, preferred_element_type=jnp.float32
    )
    read = readout.reshape(nheads, HEAD)
    field = pair_sum(jnp.sum(out * read[None, :, :], axis=(1, 2)), "heads", n_heads)
    onehot = (horizon_ids[:, None] == jnp.arange(HORIZONS, dtype=jnp.int32)[None, :]).astype(
        jnp.float32
    )
    target = jnp.sum(onehot * horizon_levels[None, :], axis=1)
    miss = field - target
    value_read = jnp.einsum("lhc,hc->hl", dec_vals.astype(jnp.float32), read, precision=high)
    dprob = miss[None, :, None] * value_read[:, None, :]
    dscore = (weights * (dprob - jnp.sum(dprob * weights, axis=2, keepdims=True))).astype(
        jnp.bfloat16
    )
    dquery = (
        (jnp.einsum("htl,lhc->thc", dscore, dec_keys, preferred_element_type=jnp.float32) * scale)
        .reshape(count, local)
        .astype(jnp.bfloat16)
    )
    grad_query = lax.psum_scatter(
        jnp.dot(enc.T, dquery, preferred_element_type=jnp.float32).astype(jnp.bfloat16),
        "picks",
        scatter_dimension=0,
        tiled=True,
    ).astype(jnp.float32)
    return (field, latents_out, grad_query)


def solution(mesh):
    in_specs = (
        P(None, ("groups", "picks")),
        P(("groups", "picks")),
        P("groups"),
        P(),
        P("picks", None, "heads"),
        P("heads", None),
        P(),
        P(None, None, "heads"),
        P(None, "heads"),
        P(None, None, "heads"),
        P("picks", "heads"),
        P("heads"),
    )
    out_specs = (P(("groups", "picks")), P("groups", "heads"), P(("groups", "picks"), "heads"))
    body = functools.partial(
        on_device,
        n_picks=mesh.shape["picks"],
        n_heads=mesh.shape["heads"],
        n_groups=mesh.shape["groups"],
    )
    return jax.shard_map(body, mesh=mesh, in_specs=in_specs, out_specs=out_specs, check_vma=False)
```

```python
import functools

import jax
import jax.numpy as jnp
from jax import lax
from jax.sharding import PartitionSpec as P

HEAD = 128
BANDS = 512
HORIZONS = 64


PI = 3.141592653589793
EPS = 1e-06
RING_MAX = 4


def encode(coords):
    freq = jnp.linspace(1.0, BANDS / 2.0, BANDS).astype(jnp.float32)
    angle = PI * freq[None, :, None] * coords[:, None, :]
    table = jnp.concatenate([jnp.sin(angle), jnp.cos(angle)], axis=0)
    return table.reshape(6 * BANDS, coords.shape[1]).T.astype(jnp.bfloat16)


def ring_gather(x, axis, n):
    if n == 1:
        return x
    if n > RING_MAX:
        return lax.all_gather(x, axis, axis=0, tiled=True)
    idx = lax.axis_index(axis)
    blocks = [x]
    for s in range(1, n):
        blocks.append(lax.ppermute(x, axis, [(i, (i - s) % n) for i in range(n)]))
    flipped = jnp.stack(blocks)
    ordered = jnp.roll(flipped, idx, axis=0)
    return ordered.reshape((n * x.shape[0],) + x.shape[1:])


def fetch_rows(kv_weight, n_picks, n_groups):
    if n_groups != 2:
        return lax.all_gather(kv_weight, "picks", axis=0, tiled=True)
    g = lax.axis_index("groups")
    rows = kv_weight.shape[0] // 2
    mine = lax.dynamic_slice_in_dim(kv_weight, g * rows, rows, 0)
    first = max(8, (2 * rows // 3) // 8 * 8)
    bounds = [(0, first), (first, rows)] if first < rows else [(0, rows)]
    own, other = [], []
    for lo, hi in bounds:
        gathered = lax.all_gather(mine[lo:hi], "picks", axis=0, tiled=False)
        own.append(gathered)
        other.append(lax.ppermute(gathered, "groups", [(0, 1), (1, 0)]))
    halves = jnp.stack([jnp.concatenate(own, axis=1), jnp.concatenate(other, axis=1)], axis=1)
    halves = jnp.roll(halves, g, axis=1)
    return halves.reshape((n_picks * kv_weight.shape[0],) + kv_weight.shape[1:])


def pair_sum(x, axis, n):
    if n != 4:
        return lax.psum(x, axis)
    x = x + lax.ppermute(x, axis, [(k, k ^ 1) for k in range(n)])
    return x + lax.ppermute(x, axis, [(k, k ^ 2) for k in range(n)])


def fetch_rows(w, n_picks, n_groups, chunks=2):
    if n_groups != 2 or n_picks > RING_MAX:
        return lax.all_gather(w, "picks", axis=0, tiled=True)
    g = lax.axis_index("groups")
    p = lax.axis_index("picks")
    rows = w.shape[0] // 2
    step = rows // chunks
    mine = lax.dynamic_slice_in_dim(w, g * rows, rows, 0)
    own, other = [], []
    for c in range(chunks):
        part = mine[c * step:(c + 1) * step]
        if own:
            part, _ = lax.optimization_barrier((part, own[-1]))
        blocks = [part] + [
            lax.ppermute(part, "picks", [(i, (i - s) % n_picks) for i in range(n_picks)])
            for s in range(1, n_picks)
        ]
        flipped = jnp.stack(blocks)
        own.append(flipped)
        other.append(lax.ppermute(flipped, "groups", [(0, 1), (1, 0)]))
    own = jnp.concatenate(own, axis=1)
    other = jnp.concatenate(other, axis=1)
    first = jnp.where(g == 0, own, other)
    second = jnp.where(g == 0, other, own)
    flipped = jnp.stack([first, second], axis=1)
    ordered = jnp.roll(flipped, p, axis=0)
    return ordered.reshape((n_picks * w.shape[0],) + w.shape[1:])


def on_device(
    coords,
    horizon_ids,
    horizon_levels,
    latents,
    kv_weight,
    cross_out,
    norm_gains,
    self_qkv,
    self_out,
    dec_kv,
    dec_query,
    readout,
    *,
    n_picks,
    n_heads,
    n_groups,
):
    high = lax.Precision.HIGHEST
    scale = HEAD ** (-0.5)
    count = coords.shape[1]
    width = latents.shape[1]
    lat_rows = latents.shape[0]
    local = kv_weight.shape[2]
    nheads = local // HEAD
    column = lax.axis_index("heads") * local
    enc = encode(coords)
    cross_full = lax.all_gather(cross_out, "heads", axis=0, tiled=True)
    piece = fetch_rows(kv_weight.reshape(kv_weight.shape[0], 2 * local), n_picks, n_groups)
    cross_full, piece = lax.optimization_barrier((cross_full, piece))
    keys_vals = jnp.dot(
        enc, piece.reshape(piece.shape[0], 2 * local), preferred_element_type=jnp.float32
    ).astype(jnp.bfloat16)
    keys = keys_vals[:, :local].reshape(count, nheads, HEAD)
    values = keys_vals[:, local:].reshape(count, nheads, HEAD)
    queries = lax.dynamic_slice_in_dim(latents, column, local, 1).reshape(lat_rows, nheads, HEAD)
    scores = jnp.einsum("lhc,thc->hlt", queries, keys, preferred_element_type=jnp.float32) * scale
    top = jnp.max(scores, axis=2)
    expo = jnp.exp(scores - top[:, :, None])
    total = jnp.sum(expo, axis=2)
    numer = jnp.einsum(
        "hlt,thc->hlc", expo.astype(jnp.bfloat16), values, preferred_element_type=jnp.float32
    )
    all_numer = lax.all_gather(numer.astype(jnp.bfloat16), "picks", axis=0, tiled=False)
    all_stats = lax.all_gather(jnp.stack([top, total]), "picks", axis=0, tiled=False)
    best = jnp.max(all_stats[:, 0], axis=0)
    factor = jnp.exp(all_stats[:, 0] - best[None])
    merged_total = jnp.sum(factor * all_stats[:, 1], axis=0)
    merged_numer = jnp.einsum(
        "phl,phlc->hlc", factor, all_numer.astype(jnp.float32), precision=high
    )
    attended = (
        (merged_numer / merged_total[:, :, None])
        .transpose(1, 0, 2)
        .reshape(lat_rows, local)
        .astype(jnp.bfloat16)
    )
    out_full = lax.all_gather(self_out, "heads", axis=1, tiled=True)
    out_full, attended = lax.optimization_barrier((out_full, attended))
    dq_local, attended = lax.optimization_barrier((dec_query, attended))
    dq_full = lax.all_gather(dq_local, "picks", axis=0, tiled=True)
    attended_full = ring_gather(attended.T, "heads", n_heads).T
    whole = latents.astype(jnp.float32) + jnp.dot(
        attended_full, cross_full, preferred_element_type=jnp.float32
    )
    power = jnp.mean(whole * whole, axis=1, keepdims=True)
    normed = (whole * lax.rsqrt(power + EPS) * norm_gains[0][None, :]).astype(jnp.bfloat16)
    state = lax.dynamic_slice_in_dim(whole, column, local, 1)
    qkv = jnp.einsum("ld,kde->kle", normed, self_qkv, preferred_element_type=jnp.float32).astype(
        jnp.bfloat16
    )
    self_q = qkv[0].reshape(lat_rows, nheads, HEAD)
    self_k = qkv[1].reshape(lat_rows, nheads, HEAD)
    self_v = qkv[2].reshape(lat_rows, nheads, HEAD)
    inner = jnp.einsum("lhc,mhc->hlm", self_q, self_k, preferred_element_type=jnp.float32) * scale
    raised = jnp.exp(inner)
    probs = (raised / jnp.sum(raised, axis=2, keepdims=True)).astype(jnp.bfloat16)
    head_out = (
        jnp.einsum("hlm,mhc->lhc", probs, self_v, preferred_element_type=jnp.float32)
        .astype(jnp.bfloat16)
        .reshape(lat_rows, local)
    )
    every_head = ring_gather(head_out.T, "heads", n_heads).T
    out_whole = whole + jnp.dot(every_head, out_full, preferred_element_type=jnp.float32)
    latents_out = lax.dynamic_slice_in_dim(out_whole, column, local, 1)
    power_two = jnp.mean(out_whole * out_whole, axis=1, keepdims=True)
    normed2 = (out_whole * lax.rsqrt(power_two + EPS) * norm_gains[1][None, :]).astype(
        jnp.bfloat16
    )
    dec = jnp.einsum("ld,kde->kle", normed2, dec_kv, preferred_element_type=jnp.float32).astype(
        jnp.bfloat16
    )
    dec_keys = dec[0].reshape(lat_rows, nheads, HEAD)
    dec_vals = dec[1].reshape(lat_rows, nheads, HEAD)
    query = jnp.dot(enc, dq_full, preferred_element_type=jnp.float32).astype(jnp.bfloat16)
    dec_q = query.reshape(count, nheads, HEAD)
    logits = jnp.einsum("thc,lhc->htl", dec_q, dec_keys, preferred_element_type=jnp.float32) * scale
    lifted = jnp.exp(logits)
    weights = lifted / jnp.sum(lifted, axis=2, keepdims=True)
    out = jnp.einsum(
        "htl,lhc->thc", weights.astype(jnp.bfloat16), dec_vals, preferred_element_type=jnp.float32
    )
    read = readout.reshape(nheads, HEAD)
    field = pair_sum(jnp.sum(out * read[None, :, :], axis=(1, 2)), "heads", n_heads)
    onehot = (horizon_ids[:, None] == jnp.arange(HORIZONS, dtype=jnp.int32)[None, :]).astype(
        jnp.float32
    )
    target = jnp.sum(onehot * horizon_levels[None, :], axis=1)
    miss = field - target
    value_read = jnp.einsum("lhc,hc->hl", dec_vals.astype(jnp.float32), read, precision=high)
    dprob = miss[None, :, None] * value_read[:, None, :]
    dscore = (weights * (dprob - jnp.sum(dprob * weights, axis=2, keepdims=True))).astype(
        jnp.bfloat16
    )
    dquery = (
        (jnp.einsum("htl,lhc->thc", dscore, dec_keys, preferred_element_type=jnp.float32) * scale)
        .reshape(count, local)
        .astype(jnp.bfloat16)
    )
    grad_query = lax.psum_scatter(
        jnp.dot(enc.T, dquery, preferred_element_type=jnp.float32).astype(jnp.bfloat16),
        "picks",
        scatter_dimension=0,
        tiled=True,
    ).astype(jnp.float32)
    return (field, latents_out, grad_query)


def solution(mesh):
    in_specs = (
        P(None, ("groups", "picks")),
        P(("groups", "picks")),
        P("groups"),
        P(),
        P("picks", None, "heads"),
        P("heads", None),
        P(),
        P(None, None, "heads"),
        P(None, "heads"),
        P(None, None, "heads"),
        P("picks", "heads"),
        P("heads"),
    )
    out_specs = (P(("groups", "picks")), P("groups", "heads"), P(("groups", "picks"), "heads"))
    body = functools.partial(
        on_device,
        n_picks=mesh.shape["picks"],
        n_heads=mesh.shape["heads"],
        n_groups=mesh.shape["groups"],
    )
    return jax.shard_map(body, mesh=mesh, in_specs=in_specs, out_specs=out_specs, check_vma=False)
```

```python
import functools

import jax
import jax.numpy as jnp
from jax import lax
from jax.sharding import PartitionSpec as P

HEAD = 128
BANDS = 512
HORIZONS = 64


PI = 3.141592653589793
EPS = 1e-06
RING_MAX = 4


def encode(coords):
    freq = jnp.linspace(1.0, BANDS / 2.0, BANDS).astype(jnp.float32)
    angle = PI * freq[None, :, None] * coords[:, None, :]
    table = jnp.concatenate([jnp.sin(angle), jnp.cos(angle)], axis=0)
    return table.reshape(6 * BANDS, coords.shape[1]).T.astype(jnp.bfloat16)


def ring_gather(x, axis, n):
    if n == 1:
        return x
    if n > RING_MAX:
        return lax.all_gather(x, axis, axis=0, tiled=True)
    idx = lax.axis_index(axis)
    blocks = [x]
    for s in range(1, n):
        blocks.append(lax.ppermute(x, axis, [(i, (i - s) % n) for i in range(n)]))
    flipped = jnp.stack(blocks)
    ordered = jnp.roll(flipped, idx, axis=0)
    return ordered.reshape((n * x.shape[0],) + x.shape[1:])


def fetch_rows(kv_weight, n_picks, n_groups):
    if n_groups != 2:
        return lax.all_gather(kv_weight, "picks", axis=0, tiled=True)
    g = lax.axis_index("groups")
    rows = kv_weight.shape[0] // 2
    mine = lax.dynamic_slice_in_dim(kv_weight, g * rows, rows, 0)
    first = max(8, (2 * rows // 3) // 8 * 8)
    bounds = [(0, first), (first, rows)] if first < rows else [(0, rows)]
    own, other = [], []
    for lo, hi in bounds:
        gathered = lax.all_gather(mine[lo:hi], "picks", axis=0, tiled=False)
        own.append(gathered)
        other.append(lax.ppermute(gathered, "groups", [(0, 1), (1, 0)]))
    halves = jnp.stack([jnp.concatenate(own, axis=1), jnp.concatenate(other, axis=1)], axis=1)
    halves = jnp.roll(halves, g, axis=1)
    return halves.reshape((n_picks * kv_weight.shape[0],) + kv_weight.shape[1:])


def pair_sum(x, axis, n):
    if n != 4:
        return lax.psum(x, axis)
    x = x + lax.ppermute(x, axis, [(k, k ^ 1) for k in range(n)])
    return x + lax.ppermute(x, axis, [(k, k ^ 2) for k in range(n)])


def fetch_rows(w, n_picks, n_groups, gate, chunks=2):
    if n_groups != 2 or n_picks > RING_MAX:
        return lax.all_gather(w, "picks", axis=0, tiled=True), gate
    g = lax.axis_index("groups")
    p = lax.axis_index("picks")
    rows = w.shape[0] // 2
    step = rows // chunks
    mine = lax.dynamic_slice_in_dim(w, g * rows, rows, 0)
    own, other = [], []
    for c in range(chunks):
        part = mine[c * step:(c + 1) * step]
        if own:
            part, _, gate = lax.optimization_barrier((part, own[-1], gate))
        blocks = [part] + [
            lax.ppermute(part, "picks", [(i, (i - s) % n_picks) for i in range(n_picks)])
            for s in range(1, n_picks)
        ]
        flipped = jnp.stack(blocks)
        own.append(flipped)
        other.append(lax.ppermute(flipped, "groups", [(0, 1), (1, 0)]))
    own = jnp.concatenate(own, axis=1)
    other = jnp.concatenate(other, axis=1)
    first = jnp.where(g == 0, own, other)
    second = jnp.where(g == 0, other, own)
    flipped = jnp.stack([first, second], axis=1)
    ordered = jnp.roll(flipped, p, axis=0)
    return ordered.reshape((n_picks * w.shape[0],) + w.shape[1:]), gate


def on_device(
    coords,
    horizon_ids,
    horizon_levels,
    latents,
    kv_weight,
    cross_out,
    norm_gains,
    self_qkv,
    self_out,
    dec_kv,
    dec_query,
    readout,
    *,
    n_picks,
    n_heads,
    n_groups,
):
    high = lax.Precision.HIGHEST
    scale = HEAD ** (-0.5)
    count = coords.shape[1]
    width = latents.shape[1]
    lat_rows = latents.shape[0]
    local = kv_weight.shape[2]
    nheads = local // HEAD
    column = lax.axis_index("heads") * local
    enc = encode(coords)
    cross_full = lax.all_gather(cross_out, "heads", axis=0, tiled=True)
    piece, enc = fetch_rows(kv_weight.reshape(kv_weight.shape[0], 2 * local), n_picks, n_groups, enc)
    out_full = lax.all_gather(self_out, "heads", axis=1, tiled=True)
    out_full, cross_full, piece = lax.optimization_barrier((out_full, cross_full, piece))
    cross_full, piece = lax.optimization_barrier((cross_full, piece))
    keys_vals = jnp.dot(
        enc, piece.reshape(piece.shape[0], 2 * local), preferred_element_type=jnp.float32
    ).astype(jnp.bfloat16)
    keys = keys_vals[:, :local].reshape(count, nheads, HEAD)
    values = keys_vals[:, local:].reshape(count, nheads, HEAD)
    queries = lax.dynamic_slice_in_dim(latents, column, local, 1).reshape(lat_rows, nheads, HEAD)
    scores = jnp.einsum("lhc,thc->hlt", queries, keys, preferred_element_type=jnp.float32) * scale
    top = jnp.max(scores, axis=2)
    expo = jnp.exp(scores - top[:, :, None])
    total = jnp.sum(expo, axis=2)
    numer = jnp.einsum(
        "hlt,thc->hlc", expo.astype(jnp.bfloat16), values, preferred_element_type=jnp.float32
    )
    all_numer = lax.all_gather(numer.astype(jnp.bfloat16), "picks", axis=0, tiled=False)
    all_stats = lax.all_gather(jnp.stack([top, total]), "picks", axis=0, tiled=False)
    best = jnp.max(all_stats[:, 0], axis=0)
    factor = jnp.exp(all_stats[:, 0] - best[None])
    merged_total = jnp.sum(factor * all_stats[:, 1], axis=0)
    merged_numer = jnp.einsum(
        "phl,phlc->hlc", factor, all_numer.astype(jnp.float32), precision=high
    )
    attended = (
        (merged_numer / merged_total[:, :, None])
        .transpose(1, 0, 2)
        .reshape(lat_rows, local)
        .astype(jnp.bfloat16)
    )
    dq_local, attended = lax.optimization_barrier((dec_query, attended))
    dq_full = lax.all_gather(dq_local, "picks", axis=0, tiled=True)
    attended_full = ring_gather(attended.T, "heads", n_heads).T
    whole = latents.astype(jnp.float32) + jnp.dot(
        attended_full, cross_full, preferred_element_type=jnp.float32
    )
    power = jnp.mean(whole * whole, axis=1, keepdims=True)
    normed = (whole * lax.rsqrt(power + EPS) * norm_gains[0][None, :]).astype(jnp.bfloat16)
    state = lax.dynamic_slice_in_dim(whole, column, local, 1)
    qkv = jnp.einsum("ld,kde->kle", normed, self_qkv, preferred_element_type=jnp.float32).astype(
        jnp.bfloat16
    )
    self_q = qkv[0].reshape(lat_rows, nheads, HEAD)
    self_k = qkv[1].reshape(lat_rows, nheads, HEAD)
    self_v = qkv[2].reshape(lat_rows, nheads, HEAD)
    inner = jnp.einsum("lhc,mhc->hlm", self_q, self_k, preferred_element_type=jnp.float32) * scale
    raised = jnp.exp(inner)
    probs = (raised / jnp.sum(raised, axis=2, keepdims=True)).astype(jnp.bfloat16)
    head_out = (
        jnp.einsum("hlm,mhc->lhc", probs, self_v, preferred_element_type=jnp.float32)
        .astype(jnp.bfloat16)
        .reshape(lat_rows, local)
    )
    every_head = ring_gather(head_out.T, "heads", n_heads).T
    out_whole = whole + jnp.dot(every_head, out_full, preferred_element_type=jnp.float32)
    latents_out = lax.dynamic_slice_in_dim(out_whole, column, local, 1)
    power_two = jnp.mean(out_whole * out_whole, axis=1, keepdims=True)
    normed2 = (out_whole * lax.rsqrt(power_two + EPS) * norm_gains[1][None, :]).astype(
        jnp.bfloat16
    )
    dec = jnp.einsum("ld,kde->kle", normed2, dec_kv, preferred_element_type=jnp.float32).astype(
        jnp.bfloat16
    )
    dec_keys = dec[0].reshape(lat_rows, nheads, HEAD)
    dec_vals = dec[1].reshape(lat_rows, nheads, HEAD)
    query = jnp.dot(enc, dq_full, preferred_element_type=jnp.float32).astype(jnp.bfloat16)
    dec_q = query.reshape(count, nheads, HEAD)
    logits = jnp.einsum("thc,lhc->htl", dec_q, dec_keys, preferred_element_type=jnp.float32) * scale
    lifted = jnp.exp(logits)
    weights = lifted / jnp.sum(lifted, axis=2, keepdims=True)
    out = jnp.einsum(
        "htl,lhc->thc", weights.astype(jnp.bfloat16), dec_vals, preferred_element_type=jnp.float32
    )
    read = readout.reshape(nheads, HEAD)
    field = pair_sum(jnp.sum(out * read[None, :, :], axis=(1, 2)), "heads", n_heads)
    onehot = (horizon_ids[:, None] == jnp.arange(HORIZONS, dtype=jnp.int32)[None, :]).astype(
        jnp.float32
    )
    target = jnp.sum(onehot * horizon_levels[None, :], axis=1)
    miss = field - target
    value_read = jnp.einsum("lhc,hc->hl", dec_vals.astype(jnp.float32), read, precision=high)
    dprob = miss[None, :, None] * value_read[:, None, :]
    dscore = (weights * (dprob - jnp.sum(dprob * weights, axis=2, keepdims=True))).astype(
        jnp.bfloat16
    )
    dquery = (
        (jnp.einsum("htl,lhc->thc", dscore, dec_keys, preferred_element_type=jnp.float32) * scale)
        .reshape(count, local)
        .astype(jnp.bfloat16)
    )
    grad_query = lax.psum_scatter(
        jnp.dot(enc.T, dquery, preferred_element_type=jnp.float32).astype(jnp.bfloat16),
        "picks",
        scatter_dimension=0,
        tiled=True,
    ).astype(jnp.float32)
    return (field, latents_out, grad_query)


def solution(mesh):
    in_specs = (
        P(None, ("groups", "picks")),
        P(("groups", "picks")),
        P("groups"),
        P(),
        P("picks", None, "heads"),
        P("heads", None),
        P(),
        P(None, None, "heads"),
        P(None, "heads"),
        P(None, None, "heads"),
        P("picks", "heads"),
        P("heads"),
    )
    out_specs = (P(("groups", "picks")), P("groups", "heads"), P(("groups", "picks"), "heads"))
    body = functools.partial(
        on_device,
        n_picks=mesh.shape["picks"],
        n_heads=mesh.shape["heads"],
        n_groups=mesh.shape["groups"],
    )
    return jax.shard_map(body, mesh=mesh, in_specs=in_specs, out_specs=out_specs, check_vma=False)
```

```python
import functools

import jax
import jax.numpy as jnp
from jax import lax
from jax.sharding import PartitionSpec as P

HEAD = 128
BANDS = 512
HORIZONS = 64


PI = 3.141592653589793
EPS = 1e-06
RING_MAX = 4


def encode(coords):
    freq = jnp.linspace(1.0, BANDS / 2.0, BANDS).astype(jnp.float32)
    angle = PI * freq[None, :, None] * coords[:, None, :]
    table = jnp.concatenate([jnp.sin(angle), jnp.cos(angle)], axis=0)
    return table.reshape(6 * BANDS, coords.shape[1]).T.astype(jnp.bfloat16)


def ring_gather(x, axis, n):
    if n == 1:
        return x
    if n > RING_MAX:
        return lax.all_gather(x, axis, axis=0, tiled=True)
    idx = lax.axis_index(axis)
    blocks = [x]
    for s in range(1, n):
        blocks.append(lax.ppermute(x, axis, [(i, (i - s) % n) for i in range(n)]))
    flipped = jnp.stack(blocks)
    ordered = jnp.roll(flipped, idx, axis=0)
    return ordered.reshape((n * x.shape[0],) + x.shape[1:])


def fetch_rows(kv_weight, n_picks, n_groups):
    if n_groups != 2:
        return lax.all_gather(kv_weight, "picks", axis=0, tiled=True)
    g = lax.axis_index("groups")
    rows = kv_weight.shape[0] // 2
    mine = lax.dynamic_slice_in_dim(kv_weight, g * rows, rows, 0)
    first = max(8, (2 * rows // 3) // 8 * 8)
    bounds = [(0, first), (first, rows)] if first < rows else [(0, rows)]
    own, other = [], []
    for lo, hi in bounds:
        gathered = lax.all_gather(mine[lo:hi], "picks", axis=0, tiled=False)
        own.append(gathered)
        other.append(lax.ppermute(gathered, "groups", [(0, 1), (1, 0)]))
    halves = jnp.stack([jnp.concatenate(own, axis=1), jnp.concatenate(other, axis=1)], axis=1)
    halves = jnp.roll(halves, g, axis=1)
    return halves.reshape((n_picks * kv_weight.shape[0],) + kv_weight.shape[1:])


def pair_sum(x, axis, n):
    if n != 4:
        return lax.psum(x, axis)
    x = x + lax.ppermute(x, axis, [(k, k ^ 1) for k in range(n)])
    return x + lax.ppermute(x, axis, [(k, k ^ 2) for k in range(n)])


def pair_gather(x, axis, n):
    near = lax.ppermute(x, axis, [(k, k ^ 1) for k in range(n)])
    far = lax.ppermute(x, axis, [(k, k ^ 2) for k in range(n)])
    far_near = lax.ppermute(far, axis, [(k, k ^ 1) for k in range(n)])
    return jnp.concatenate([x, near, far, far_near], axis=0)


def xor_blocks(x, idx, n):
    blocks = x.reshape((n, x.shape[0] // n) + x.shape[1:])
    return jnp.take(blocks, jnp.arange(n) ^ idx, axis=0).reshape(x.shape)


def on_device(
    coords,
    horizon_ids,
    horizon_levels,
    latents,
    kv_weight,
    cross_out,
    norm_gains,
    self_qkv,
    self_out,
    dec_kv,
    dec_query,
    readout,
    *,
    n_picks,
    n_heads,
    n_groups,
):
    high = lax.Precision.HIGHEST
    scale = HEAD ** (-0.5)
    count = coords.shape[1]
    width = latents.shape[1]
    lat_rows = latents.shape[0]
    local = kv_weight.shape[2]
    nheads = local // HEAD
    column = lax.axis_index("heads") * local
    enc = encode(coords)
    paired = n_heads == 4
    if paired:
        cross_full = pair_gather(cross_out, "heads", n_heads)
    else:
        cross_full = ring_gather(cross_out, "heads", n_heads)
    piece = lax.all_gather(
        kv_weight.reshape(kv_weight.shape[0], 2 * local), "picks", axis=0, tiled=True
    )
    cross_full, piece = lax.optimization_barrier((cross_full, piece))
    keys_vals = jnp.dot(
        enc, piece.reshape(piece.shape[0], 2 * local), preferred_element_type=jnp.float32
    ).astype(jnp.bfloat16)
    keys = keys_vals[:, :local].reshape(count, nheads, HEAD)
    values = keys_vals[:, local:].reshape(count, nheads, HEAD)
    queries = lax.dynamic_slice_in_dim(latents, column, local, 1).reshape(lat_rows, nheads, HEAD)
    scores = jnp.einsum("lhc,thc->hlt", queries, keys, preferred_element_type=jnp.float32) * scale
    top = jnp.max(scores, axis=2)
    expo = jnp.exp(scores - top[:, :, None])
    total = jnp.sum(expo, axis=2)
    numer = jnp.einsum(
        "hlt,thc->hlc", expo.astype(jnp.bfloat16), values, preferred_element_type=jnp.float32
    )
    all_numer = lax.all_gather(numer.astype(jnp.bfloat16), "picks", axis=0, tiled=False)
    all_stats = lax.all_gather(jnp.stack([top, total]), "picks", axis=0, tiled=False)
    best = jnp.max(all_stats[:, 0], axis=0)
    factor = jnp.exp(all_stats[:, 0] - best[None])
    merged_total = jnp.sum(factor * all_stats[:, 1], axis=0)
    merged_numer = jnp.einsum(
        "phl,phlc->hlc", factor, all_numer.astype(jnp.float32), precision=high
    )
    attended = (
        (merged_numer / merged_total[:, :, None])
        .transpose(1, 0, 2)
        .reshape(lat_rows, local)
        .astype(jnp.bfloat16)
    )
    out_full = ring_gather(self_out.T, "heads", n_heads).T
    if paired:
        out_full = xor_blocks(out_full, lax.axis_index("heads"), n_heads)
    out_full, attended = lax.optimization_barrier((out_full, attended))
    dq_local, attended = lax.optimization_barrier((dec_query, attended))
    dq_full = lax.all_gather(dq_local, "picks", axis=0, tiled=True)
    head_gather = pair_gather if paired else ring_gather
    attended_full = head_gather(attended.T, "heads", n_heads).T
    whole = latents.astype(jnp.float32) + jnp.dot(
        attended_full, cross_full, preferred_element_type=jnp.float32
    )
    power = jnp.mean(whole * whole, axis=1, keepdims=True)
    normed = (whole * lax.rsqrt(power + EPS) * norm_gains[0][None, :]).astype(jnp.bfloat16)
    state = lax.dynamic_slice_in_dim(whole, column, local, 1)
    qkv = jnp.einsum("ld,kde->kle", normed, self_qkv, preferred_element_type=jnp.float32).astype(
        jnp.bfloat16
    )
    self_q = qkv[0].reshape(lat_rows, nheads, HEAD)
    self_k = qkv[1].reshape(lat_rows, nheads, HEAD)
    self_v = qkv[2].reshape(lat_rows, nheads, HEAD)
    inner = jnp.einsum("lhc,mhc->hlm", self_q, self_k, preferred_element_type=jnp.float32) * scale
    raised = jnp.exp(inner)
    probs = (raised / jnp.sum(raised, axis=2, keepdims=True)).astype(jnp.bfloat16)
    head_out = (
        jnp.einsum("hlm,mhc->lhc", probs, self_v, preferred_element_type=jnp.float32)
        .astype(jnp.bfloat16)
        .reshape(lat_rows, local)
    )
    every_head = head_gather(head_out.T, "heads", n_heads).T
    out_whole = whole + jnp.dot(every_head, out_full, preferred_element_type=jnp.float32)
    latents_out = lax.dynamic_slice_in_dim(out_whole, column, local, 1)
    power_two = jnp.mean(out_whole * out_whole, axis=1, keepdims=True)
    normed2 = (out_whole * lax.rsqrt(power_two + EPS) * norm_gains[1][None, :]).astype(
        jnp.bfloat16
    )
    dec = jnp.einsum("ld,kde->kle", normed2, dec_kv, preferred_element_type=jnp.float32).astype(
        jnp.bfloat16
    )
    dec_keys = dec[0].reshape(lat_rows, nheads, HEAD)
    dec_vals = dec[1].reshape(lat_rows, nheads, HEAD)
    query = jnp.dot(enc, dq_full, preferred_element_type=jnp.float32).astype(jnp.bfloat16)
    dec_q = query.reshape(count, nheads, HEAD)
    logits = jnp.einsum("thc,lhc->htl", dec_q, dec_keys, preferred_element_type=jnp.float32) * scale
    lifted = jnp.exp(logits)
    weights = lifted / jnp.sum(lifted, axis=2, keepdims=True)
    out = jnp.einsum(
        "htl,lhc->thc", weights.astype(jnp.bfloat16), dec_vals, preferred_element_type=jnp.float32
    )
    read = readout.reshape(nheads, HEAD)
    field = pair_sum(jnp.sum(out * read[None, :, :], axis=(1, 2)), "heads", n_heads)
    onehot = (horizon_ids[:, None] == jnp.arange(HORIZONS, dtype=jnp.int32)[None, :]).astype(
        jnp.float32
    )
    target = jnp.sum(onehot * horizon_levels[None, :], axis=1)
    miss = field - target
    value_read = jnp.einsum("lhc,hc->hl", dec_vals.astype(jnp.float32), read, precision=high)
    dprob = miss[None, :, None] * value_read[:, None, :]
    dscore = (weights * (dprob - jnp.sum(dprob * weights, axis=2, keepdims=True))).astype(
        jnp.bfloat16
    )
    dquery = (
        (jnp.einsum("htl,lhc->thc", dscore, dec_keys, preferred_element_type=jnp.float32) * scale)
        .reshape(count, local)
        .astype(jnp.bfloat16)
    )
    grad_query = lax.psum_scatter(
        jnp.dot(enc.T, dquery, preferred_element_type=jnp.float32).astype(jnp.bfloat16),
        "picks",
        scatter_dimension=0,
        tiled=True,
    ).astype(jnp.float32)
    return (field, latents_out, grad_query)


def solution(mesh):
    in_specs = (
        P(None, ("groups", "picks")),
        P(("groups", "picks")),
        P("groups"),
        P(),
        P("picks", None, "heads"),
        P("heads", None),
        P(),
        P(None, None, "heads"),
        P(None, "heads"),
        P(None, None, "heads"),
        P("picks", "heads"),
        P("heads"),
    )
    out_specs = (P(("groups", "picks")), P("groups", "heads"), P(("groups", "picks"), "heads"))
    body = functools.partial(
        on_device,
        n_picks=mesh.shape["picks"],
        n_heads=mesh.shape["heads"],
        n_groups=mesh.shape["groups"],
    )
    return jax.shard_map(body, mesh=mesh, in_specs=in_specs, out_specs=out_specs, check_vma=False)
```

```python
import functools

import jax
import jax.numpy as jnp
from jax import lax
from jax.sharding import PartitionSpec as P

HEAD = 128
BANDS = 512
HORIZONS = 64


PI = 3.141592653589793
EPS = 1e-06
RING_MAX = 4


def encode(coords):
    freq = jnp.linspace(1.0, BANDS / 2.0, BANDS).astype(jnp.float32)
    angle = PI * freq[None, :, None] * coords[:, None, :]
    table = jnp.concatenate([jnp.sin(angle), jnp.cos(angle)], axis=0)
    return table.reshape(6 * BANDS, coords.shape[1]).T.astype(jnp.bfloat16)


def ring_gather(x, axis, n):
    if n == 1:
        return x
    if n > RING_MAX:
        return lax.all_gather(x, axis, axis=0, tiled=True)
    idx = lax.axis_index(axis)
    blocks = [x]
    for s in range(1, n):
        blocks.append(lax.ppermute(x, axis, [(i, (i - s) % n) for i in range(n)]))
    flipped = jnp.stack(blocks)
    ordered = jnp.roll(flipped, idx, axis=0)
    return ordered.reshape((n * x.shape[0],) + x.shape[1:])


def fetch_rows(kv_weight, n_picks, n_groups):
    if n_groups != 2:
        return lax.all_gather(kv_weight, "picks", axis=0, tiled=True)
    g = lax.axis_index("groups")
    rows = kv_weight.shape[0] // 2
    mine = lax.dynamic_slice_in_dim(kv_weight, g * rows, rows, 0)
    first = max(8, (2 * rows // 3) // 8 * 8)
    bounds = [(0, first), (first, rows)] if first < rows else [(0, rows)]
    own, other = [], []
    for lo, hi in bounds:
        gathered = lax.all_gather(mine[lo:hi], "picks", axis=0, tiled=False)
        own.append(gathered)
        other.append(lax.ppermute(gathered, "groups", [(0, 1), (1, 0)]))
    halves = jnp.stack([jnp.concatenate(own, axis=1), jnp.concatenate(other, axis=1)], axis=1)
    halves = jnp.roll(halves, g, axis=1)
    return halves.reshape((n_picks * kv_weight.shape[0],) + kv_weight.shape[1:])


def pair_sum(x, axis, n):
    if n != 4:
        return lax.psum(x, axis)
    x = x + lax.ppermute(x, axis, [(k, k ^ 1) for k in range(n)])
    return x + lax.ppermute(x, axis, [(k, k ^ 2) for k in range(n)])


def pair_gather(x, axis, n):
    near = lax.ppermute(x, axis, [(k, k ^ 1) for k in range(n)])
    far = lax.ppermute(x, axis, [(k, k ^ 2) for k in range(n)])
    far_near = lax.ppermute(far, axis, [(k, k ^ 1) for k in range(n)])
    return jnp.concatenate([x, near, far, far_near], axis=0)


def xor_blocks(x, idx, n):
    blocks = x.reshape((n, x.shape[0] // n) + x.shape[1:])
    return jnp.take(blocks, jnp.arange(n) ^ idx, axis=0).reshape(x.shape)


def on_device(
    coords,
    horizon_ids,
    horizon_levels,
    latents,
    kv_weight,
    cross_out,
    norm_gains,
    self_qkv,
    self_out,
    dec_kv,
    dec_query,
    readout,
    *,
    n_picks,
    n_heads,
    n_groups,
):
    high = lax.Precision.HIGHEST
    scale = HEAD ** (-0.5)
    count = coords.shape[1]
    width = latents.shape[1]
    lat_rows = latents.shape[0]
    local = kv_weight.shape[2]
    nheads = local // HEAD
    column = lax.axis_index("heads") * local
    enc = encode(coords)
    paired = n_heads == 4
    if paired:
        cross_full = pair_gather(cross_out, "heads", n_heads)
    else:
        cross_full = ring_gather(cross_out, "heads", n_heads)
    piece = lax.all_gather(
        kv_weight.reshape(kv_weight.shape[0], 2 * local), "picks", axis=0, tiled=True
    )
    out_full = ring_gather(self_out.T, "heads", n_heads).T
    if paired:
        out_full = xor_blocks(out_full, lax.axis_index("heads"), n_heads)
    out_full, cross_full, piece = lax.optimization_barrier((out_full, cross_full, piece))
    keys_vals = jnp.dot(
        enc, piece.reshape(piece.shape[0], 2 * local), preferred_element_type=jnp.float32
    ).astype(jnp.bfloat16)
    keys = keys_vals[:, :local].reshape(count, nheads, HEAD)
    values = keys_vals[:, local:].reshape(count, nheads, HEAD)
    queries = lax.dynamic_slice_in_dim(latents, column, local, 1).reshape(lat_rows, nheads, HEAD)
    scores = jnp.einsum("lhc,thc->hlt", queries, keys, preferred_element_type=jnp.float32) * scale
    top = jnp.max(scores, axis=2)
    expo = jnp.exp(scores - top[:, :, None])
    total = jnp.sum(expo, axis=2)
    numer = jnp.einsum(
        "hlt,thc->hlc", expo.astype(jnp.bfloat16), values, preferred_element_type=jnp.float32
    )
    all_numer = lax.all_gather(numer.astype(jnp.bfloat16), "picks", axis=0, tiled=False)
    all_stats = lax.all_gather(jnp.stack([top, total]), "picks", axis=0, tiled=False)
    best = jnp.max(all_stats[:, 0], axis=0)
    factor = jnp.exp(all_stats[:, 0] - best[None])
    merged_total = jnp.sum(factor * all_stats[:, 1], axis=0)
    merged_numer = jnp.einsum(
        "phl,phlc->hlc", factor, all_numer.astype(jnp.float32), precision=high
    )
    attended = (
        (merged_numer / merged_total[:, :, None])
        .transpose(1, 0, 2)
        .reshape(lat_rows, local)
        .astype(jnp.bfloat16)
    )
    dq_local, attended = lax.optimization_barrier((dec_query, attended))
    dq_full = lax.all_gather(dq_local, "picks", axis=0, tiled=True)
    head_gather = pair_gather if paired else ring_gather
    attended_full = head_gather(attended.T, "heads", n_heads).T
    whole = latents.astype(jnp.float32) + jnp.dot(
        attended_full, cross_full, preferred_element_type=jnp.float32
    )
    power = jnp.mean(whole * whole, axis=1, keepdims=True)
    normed = (whole * lax.rsqrt(power + EPS) * norm_gains[0][None, :]).astype(jnp.bfloat16)
    state = lax.dynamic_slice_in_dim(whole, column, local, 1)
    qkv = jnp.einsum("ld,kde->kle", normed, self_qkv, preferred_element_type=jnp.float32).astype(
        jnp.bfloat16
    )
    self_q = qkv[0].reshape(lat_rows, nheads, HEAD)
    self_k = qkv[1].reshape(lat_rows, nheads, HEAD)
    self_v = qkv[2].reshape(lat_rows, nheads, HEAD)
    inner = jnp.einsum("lhc,mhc->hlm", self_q, self_k, preferred_element_type=jnp.float32) * scale
    raised = jnp.exp(inner)
    probs = (raised / jnp.sum(raised, axis=2, keepdims=True)).astype(jnp.bfloat16)
    head_out = (
        jnp.einsum("hlm,mhc->lhc", probs, self_v, preferred_element_type=jnp.float32)
        .astype(jnp.bfloat16)
        .reshape(lat_rows, local)
    )
    every_head = head_gather(head_out.T, "heads", n_heads).T
    dq_full, every_head = lax.optimization_barrier((dq_full, every_head))
    out_whole = whole + jnp.dot(every_head, out_full, preferred_element_type=jnp.float32)
    latents_out = lax.dynamic_slice_in_dim(out_whole, column, local, 1)
    power_two = jnp.mean(out_whole * out_whole, axis=1, keepdims=True)
    normed2 = (out_whole * lax.rsqrt(power_two + EPS) * norm_gains[1][None, :]).astype(
        jnp.bfloat16
    )
    dec = jnp.einsum("ld,kde->kle", normed2, dec_kv, preferred_element_type=jnp.float32).astype(
        jnp.bfloat16
    )
    dec_keys = dec[0].reshape(lat_rows, nheads, HEAD)
    dec_vals = dec[1].reshape(lat_rows, nheads, HEAD)
    query = jnp.dot(enc, dq_full, preferred_element_type=jnp.float32).astype(jnp.bfloat16)
    dec_q = query.reshape(count, nheads, HEAD)
    logits = jnp.einsum("thc,lhc->htl", dec_q, dec_keys, preferred_element_type=jnp.float32) * scale
    lifted = jnp.exp(logits)
    weights = lifted / jnp.sum(lifted, axis=2, keepdims=True)
    out = jnp.einsum(
        "htl,lhc->thc", weights.astype(jnp.bfloat16), dec_vals, preferred_element_type=jnp.float32
    )
    read = readout.reshape(nheads, HEAD)
    field = pair_sum(jnp.sum(out * read[None, :, :], axis=(1, 2)), "heads", n_heads)
    onehot = (horizon_ids[:, None] == jnp.arange(HORIZONS, dtype=jnp.int32)[None, :]).astype(
        jnp.float32
    )
    target = jnp.sum(onehot * horizon_levels[None, :], axis=1)
    miss = field - target
    value_read = jnp.einsum("lhc,hc->hl", dec_vals.astype(jnp.float32), read, precision=high)
    dprob = miss[None, :, None] * value_read[:, None, :]
    dscore = (weights * (dprob - jnp.sum(dprob * weights, axis=2, keepdims=True))).astype(
        jnp.bfloat16
    )
    dquery = (
        (jnp.einsum("htl,lhc->thc", dscore, dec_keys, preferred_element_type=jnp.float32) * scale)
        .reshape(count, local)
        .astype(jnp.bfloat16)
    )
    grad_query = lax.psum_scatter(
        jnp.dot(enc.T, dquery, preferred_element_type=jnp.float32).astype(jnp.bfloat16),
        "picks",
        scatter_dimension=0,
        tiled=True,
    ).astype(jnp.float32)
    return (field, latents_out, grad_query)


def solution(mesh):
    in_specs = (
        P(None, ("groups", "picks")),
        P(("groups", "picks")),
        P("groups"),
        P(),
        P("picks", None, "heads"),
        P("heads", None),
        P(),
        P(None, None, "heads"),
        P(None, "heads"),
        P(None, None, "heads"),
        P("picks", "heads"),
        P("heads"),
    )
    out_specs = (P(("groups", "picks")), P("groups", "heads"), P(("groups", "picks"), "heads"))
    body = functools.partial(
        on_device,
        n_picks=mesh.shape["picks"],
        n_heads=mesh.shape["heads"],
        n_groups=mesh.shape["groups"],
    )
    return jax.shard_map(body, mesh=mesh, in_specs=in_specs, out_specs=out_specs, check_vma=False)
```

```python
import functools

import jax
import jax.numpy as jnp
from jax import lax
from jax.sharding import PartitionSpec as P

HEAD = 128
BANDS = 512
HORIZONS = 64


PI = 3.141592653589793
EPS = 1e-06
RING_MAX = 4


def encode(coords):
    freq = jnp.linspace(1.0, BANDS / 2.0, BANDS).astype(jnp.float32)
    angle = PI * freq[None, :, None] * coords[:, None, :]
    table = jnp.concatenate([jnp.sin(angle), jnp.cos(angle)], axis=0)
    return table.reshape(6 * BANDS, coords.shape[1]).T.astype(jnp.bfloat16)


def ring_gather(x, axis, n):
    if n == 1:
        return x
    if n > RING_MAX:
        return lax.all_gather(x, axis, axis=0, tiled=True)
    idx = lax.axis_index(axis)
    blocks = [x]
    for s in range(1, n):
        blocks.append(lax.ppermute(x, axis, [(i, (i - s) % n) for i in range(n)]))
    flipped = jnp.stack(blocks)
    ordered = jnp.roll(flipped, idx, axis=0)
    return ordered.reshape((n * x.shape[0],) + x.shape[1:])


def fetch_rows(kv_weight, n_picks, n_groups):
    if n_groups != 2:
        return lax.all_gather(kv_weight, "picks", axis=0, tiled=True)
    g = lax.axis_index("groups")
    rows = kv_weight.shape[0] // 2
    mine = lax.dynamic_slice_in_dim(kv_weight, g * rows, rows, 0)
    first = max(8, (2 * rows // 3) // 8 * 8)
    bounds = [(0, first), (first, rows)] if first < rows else [(0, rows)]
    own, other = [], []
    for lo, hi in bounds:
        gathered = lax.all_gather(mine[lo:hi], "picks", axis=0, tiled=False)
        own.append(gathered)
        other.append(lax.ppermute(gathered, "groups", [(0, 1), (1, 0)]))
    halves = jnp.stack([jnp.concatenate(own, axis=1), jnp.concatenate(other, axis=1)], axis=1)
    halves = jnp.roll(halves, g, axis=1)
    return halves.reshape((n_picks * kv_weight.shape[0],) + kv_weight.shape[1:])


def pair_sum(x, axis, n):
    if n != 4:
        return lax.psum(x, axis)
    x = x + lax.ppermute(x, axis, [(k, k ^ 1) for k in range(n)])
    return x + lax.ppermute(x, axis, [(k, k ^ 2) for k in range(n)])


def on_device(
    coords,
    horizon_ids,
    horizon_levels,
    latents,
    kv_weight,
    cross_out,
    norm_gains,
    self_qkv,
    self_out,
    dec_kv,
    dec_query,
    readout,
    *,
    n_picks,
    n_heads,
    n_groups,
):
    high = lax.Precision.HIGHEST
    scale = HEAD ** (-0.5)
    count = coords.shape[1]
    width = latents.shape[1]
    lat_rows = latents.shape[0]
    local = kv_weight.shape[2]
    nheads = local // HEAD
    column = lax.axis_index("heads") * local
    enc = encode(coords)
    cross_full = ring_gather(cross_out, "heads", n_heads)
    piece = lax.all_gather(
        kv_weight.reshape(kv_weight.shape[0], 2 * local), "picks", axis=0, tiled=True
    )
    cross_full, piece = lax.optimization_barrier((cross_full, piece))
    keys_vals = jnp.dot(
        enc, piece.reshape(piece.shape[0], 2 * local), preferred_element_type=jnp.float32
    ).astype(jnp.bfloat16)
    keys = keys_vals[:, :local].reshape(count, nheads, HEAD)
    values = keys_vals[:, local:].reshape(count, nheads, HEAD)
    queries = lax.dynamic_slice_in_dim(latents, column, local, 1).reshape(lat_rows, nheads, HEAD)
    scores = jnp.einsum("lhc,thc->hlt", queries, keys, preferred_element_type=jnp.float32) * scale
    top = jnp.max(scores, axis=2)
    expo = jnp.exp(scores - top[:, :, None])
    total = jnp.sum(expo, axis=2)
    numer = jnp.einsum(
        "hlt,thc->hlc", expo.astype(jnp.bfloat16), values, preferred_element_type=jnp.float32
    )
    all_numer = lax.all_gather(numer.astype(jnp.bfloat16), "picks", axis=0, tiled=False)
    all_stats = lax.all_gather(jnp.stack([top, total]), "picks", axis=0, tiled=False)
    best = jnp.max(all_stats[:, 0], axis=0)
    factor = jnp.exp(all_stats[:, 0] - best[None])
    merged_total = jnp.sum(factor * all_stats[:, 1], axis=0)
    merged_numer = jnp.einsum(
        "phl,phlc->hlc", factor, all_numer.astype(jnp.float32), precision=high
    )
    attended = (
        (merged_numer / merged_total[:, :, None])
        .transpose(1, 0, 2)
        .reshape(lat_rows, local)
        .astype(jnp.bfloat16)
    )
    out_full = ring_gather(self_out.T, "heads", n_heads).T
    out_full, attended = lax.optimization_barrier((out_full, attended))
    dq_local, attended = lax.optimization_barrier((dec_query, attended))
    dq_full = lax.all_gather(dq_local, "picks", axis=0, tiled=True)
    attended_full = ring_gather(attended.T, "heads", n_heads).T
    whole = latents.astype(jnp.float32) + jnp.dot(
        attended_full, cross_full, preferred_element_type=jnp.float32
    )
    power = jnp.mean(whole * whole, axis=1, keepdims=True)
    normed = (whole * lax.rsqrt(power + EPS) * norm_gains[0][None, :]).astype(jnp.bfloat16)
    state = lax.dynamic_slice_in_dim(whole, column, local, 1)
    qkv = jnp.einsum("ld,kde->kle", normed, self_qkv, preferred_element_type=jnp.float32).astype(
        jnp.bfloat16
    )
    self_q = qkv[0].reshape(lat_rows, nheads, HEAD)
    self_k = qkv[1].reshape(lat_rows, nheads, HEAD)
    self_v = qkv[2].reshape(lat_rows, nheads, HEAD)
    inner = jnp.einsum("lhc,mhc->hlm", self_q, self_k, preferred_element_type=jnp.float32) * scale
    raised = jnp.exp(inner)
    probs = (raised / jnp.sum(raised, axis=2, keepdims=True)).astype(jnp.bfloat16)
    head_out = (
        jnp.einsum("hlm,mhc->lhc", probs, self_v, preferred_element_type=jnp.float32)
        .astype(jnp.bfloat16)
        .reshape(lat_rows, local)
    )
    every_head = ring_gather(head_out.T, "heads", n_heads).T
    out_whole = whole + jnp.dot(every_head, out_full, preferred_element_type=jnp.float32)
    latents_out = lax.dynamic_slice_in_dim(out_whole, column, local, 1)
    power_two = jnp.mean(out_whole * out_whole, axis=1, keepdims=True)
    normed2 = (out_whole * lax.rsqrt(power_two + EPS) * norm_gains[1][None, :]).astype(
        jnp.bfloat16
    )
    dec = jnp.einsum("ld,kde->kle", normed2, dec_kv, preferred_element_type=jnp.float32).astype(
        jnp.bfloat16
    )
    dec_keys = dec[0].reshape(lat_rows, nheads, HEAD)
    dec_vals = dec[1].reshape(lat_rows, nheads, HEAD)
    query = jnp.dot(enc, dq_full, preferred_element_type=jnp.float32).astype(jnp.bfloat16)
    dec_q = query.reshape(count, nheads, HEAD)
    logits = jnp.einsum("thc,lhc->htl", dec_q, dec_keys, preferred_element_type=jnp.float32) * scale
    lifted = jnp.exp(logits)
    weights = lifted / jnp.sum(lifted, axis=2, keepdims=True)
    out = jnp.einsum(
        "htl,lhc->thc", weights.astype(jnp.bfloat16), dec_vals, preferred_element_type=jnp.float32
    )
    read = readout.reshape(nheads, HEAD)
    onehot = (horizon_ids[:, None] == jnp.arange(HORIZONS, dtype=jnp.int32)[None, :]).astype(
        jnp.float32
    )
    target = jnp.sum(onehot * horizon_levels[None, :], axis=1)
    value_read = jnp.einsum("lhc,hc->hl", dec_vals.astype(jnp.float32), read, precision=high)
    lever = (
        weights
        * (
            value_read[:, None, :]
            - jnp.sum(value_read[:, None, :] * weights, axis=2, keepdims=True)
        )
    ).astype(jnp.bfloat16)
    pull = jnp.einsum("htl,lhc->thc", lever, dec_keys, preferred_element_type=jnp.float32) * scale
    field = pair_sum(jnp.sum(out * read[None, :, :], axis=(1, 2)), "heads", n_heads)
    miss = field - target
    dquery = (miss[:, None, None] * pull).reshape(count, local).astype(jnp.bfloat16)
    grad_query = lax.psum_scatter(
        jnp.dot(enc.T, dquery, preferred_element_type=jnp.float32).astype(jnp.bfloat16),
        "picks",
        scatter_dimension=0,
        tiled=True,
    ).astype(jnp.float32)
    return (field, latents_out, grad_query)


def solution(mesh):
    in_specs = (
        P(None, ("groups", "picks")),
        P(("groups", "picks")),
        P("groups"),
        P(),
        P("picks", None, "heads"),
        P("heads", None),
        P(),
        P(None, None, "heads"),
        P(None, "heads"),
        P(None, None, "heads"),
        P("picks", "heads"),
        P("heads"),
    )
    out_specs = (P(("groups", "picks")), P("groups", "heads"), P(("groups", "picks"), "heads"))
    body = functools.partial(
        on_device,
        n_picks=mesh.shape["picks"],
        n_heads=mesh.shape["heads"],
        n_groups=mesh.shape["groups"],
    )
    return jax.shard_map(body, mesh=mesh, in_specs=in_specs, out_specs=out_specs, check_vma=False)
```

```python
import functools

import jax
import jax.numpy as jnp
from jax import lax
from jax.sharding import PartitionSpec as P

HEAD = 128
BANDS = 512
HORIZONS = 64


PI = 3.141592653589793
EPS = 1e-06
RING_MAX = 4


def encode(coords):
    freq = jnp.linspace(1.0, BANDS / 2.0, BANDS).astype(jnp.float32)
    angle = PI * freq[None, :, None] * coords[:, None, :]
    table = jnp.concatenate([jnp.sin(angle), jnp.cos(angle)], axis=0)
    return table.reshape(6 * BANDS, coords.shape[1]).T.astype(jnp.bfloat16)


def ring_gather(x, axis, n, take=False):
    if n == 1:
        return x
    if n > RING_MAX:
        return lax.all_gather(x, axis, axis=0, tiled=True)
    idx = lax.axis_index(axis)
    blocks = [x]
    for s in range(1, n):
        blocks.append(lax.ppermute(x, axis, [(i, (i - s) % n) for i in range(n)]))
    flipped = jnp.stack(blocks)
    if take:
        ordered = jnp.take(flipped, (jnp.arange(n) - idx) % n, axis=0)
    else:
        ordered = jnp.roll(flipped, idx, axis=0)
    return ordered.reshape((n * x.shape[0],) + x.shape[1:])


def fetch_rows(kv_weight, n_picks, n_groups):
    if n_groups != 2:
        return lax.all_gather(kv_weight, "picks", axis=0, tiled=True)
    g = lax.axis_index("groups")
    rows = kv_weight.shape[0] // 2
    mine = lax.dynamic_slice_in_dim(kv_weight, g * rows, rows, 0)
    first = max(8, (2 * rows // 3) // 8 * 8)
    bounds = [(0, first), (first, rows)] if first < rows else [(0, rows)]
    own, other = [], []
    for lo, hi in bounds:
        gathered = lax.all_gather(mine[lo:hi], "picks", axis=0, tiled=False)
        own.append(gathered)
        other.append(lax.ppermute(gathered, "groups", [(0, 1), (1, 0)]))
    halves = jnp.stack([jnp.concatenate(own, axis=1), jnp.concatenate(other, axis=1)], axis=1)
    halves = jnp.roll(halves, g, axis=1)
    return halves.reshape((n_picks * kv_weight.shape[0],) + kv_weight.shape[1:])


def pair_sum(x, axis, n):
    if n != 4:
        return lax.psum(x, axis)
    x = x + lax.ppermute(x, axis, [(k, k ^ 1) for k in range(n)])
    return x + lax.ppermute(x, axis, [(k, k ^ 2) for k in range(n)])


def on_device(
    coords,
    horizon_ids,
    horizon_levels,
    latents,
    kv_weight,
    cross_out,
    norm_gains,
    self_qkv,
    self_out,
    dec_kv,
    dec_query,
    readout,
    *,
    n_picks,
    n_heads,
    n_groups,
):
    high = lax.Precision.HIGHEST
    scale = HEAD ** (-0.5)
    count = coords.shape[1]
    width = latents.shape[1]
    lat_rows = latents.shape[0]
    local = kv_weight.shape[2]
    nheads = local // HEAD
    column = lax.axis_index("heads") * local
    enc = encode(coords)
    cross_full = ring_gather(cross_out, "heads", n_heads, take=True)
    key_rows = lax.all_gather(kv_weight[:, 0, :], "picks", axis=0, tiled=True)
    value_rows = lax.all_gather(kv_weight[:, 1, :], "picks", axis=0, tiled=True)
    cross_full, value_rows = lax.optimization_barrier((cross_full, value_rows))
    keys = (
        jnp.dot(enc, key_rows, preferred_element_type=jnp.float32)
        .astype(jnp.bfloat16)
        .reshape(count, nheads, HEAD)
    )
    values = (
        jnp.dot(enc, value_rows, preferred_element_type=jnp.float32)
        .astype(jnp.bfloat16)
        .reshape(count, nheads, HEAD)
    )
    queries = lax.dynamic_slice_in_dim(latents, column, local, 1).reshape(lat_rows, nheads, HEAD)
    scores = jnp.einsum("lhc,thc->hlt", queries, keys, preferred_element_type=jnp.float32) * scale
    top = jnp.max(scores, axis=2)
    expo = jnp.exp(scores - top[:, :, None])
    total = jnp.sum(expo, axis=2)
    numer = jnp.einsum(
        "hlt,thc->hlc", expo.astype(jnp.bfloat16), values, preferred_element_type=jnp.float32
    )
    all_numer = lax.all_gather(numer.astype(jnp.bfloat16), "picks", axis=0, tiled=False)
    all_stats = lax.all_gather(jnp.stack([top, total]), "picks", axis=0, tiled=False)
    best = jnp.max(all_stats[:, 0], axis=0)
    factor = jnp.exp(all_stats[:, 0] - best[None])
    merged_total = jnp.sum(factor * all_stats[:, 1], axis=0)
    merged_numer = jnp.einsum(
        "phl,phlc->hlc", factor, all_numer.astype(jnp.float32), precision=high
    )
    attended = (
        (merged_numer / merged_total[:, :, None])
        .transpose(1, 0, 2)
        .reshape(lat_rows, local)
        .astype(jnp.bfloat16)
    )
    out_full = ring_gather(self_out.T, "heads", n_heads, take=True).T
    out_full, attended = lax.optimization_barrier((out_full, attended))
    dq_local, attended = lax.optimization_barrier((dec_query, attended))
    dq_full = lax.all_gather(dq_local, "picks", axis=0, tiled=True)
    attended_full = ring_gather(attended.T, "heads", n_heads).T
    whole = latents.astype(jnp.float32) + jnp.dot(
        attended_full, cross_full, preferred_element_type=jnp.float32
    )
    power = jnp.mean(whole * whole, axis=1, keepdims=True)
    normed = (whole * lax.rsqrt(power + EPS) * norm_gains[0][None, :]).astype(jnp.bfloat16)
    state = lax.dynamic_slice_in_dim(whole, column, local, 1)
    qkv = jnp.einsum("ld,kde->kle", normed, self_qkv, preferred_element_type=jnp.float32).astype(
        jnp.bfloat16
    )
    self_q = qkv[0].reshape(lat_rows, nheads, HEAD)
    self_k = qkv[1].reshape(lat_rows, nheads, HEAD)
    self_v = qkv[2].reshape(lat_rows, nheads, HEAD)
    inner = jnp.einsum("lhc,mhc->hlm", self_q, self_k, preferred_element_type=jnp.float32) * scale
    raised = jnp.exp(inner)
    probs = (raised / jnp.sum(raised, axis=2, keepdims=True)).astype(jnp.bfloat16)
    head_out = (
        jnp.einsum("hlm,mhc->lhc", probs, self_v, preferred_element_type=jnp.float32)
        .astype(jnp.bfloat16)
        .reshape(lat_rows, local)
    )
    every_head = ring_gather(head_out.T, "heads", n_heads).T
    out_whole = whole + jnp.dot(every_head, out_full, preferred_element_type=jnp.float32)
    latents_out = lax.dynamic_slice_in_dim(out_whole, column, local, 1)
    power_two = jnp.mean(out_whole * out_whole, axis=1, keepdims=True)
    normed2 = (out_whole * lax.rsqrt(power_two + EPS) * norm_gains[1][None, :]).astype(
        jnp.bfloat16
    )
    dec = jnp.einsum("ld,kde->kle", normed2, dec_kv, preferred_element_type=jnp.float32).astype(
        jnp.bfloat16
    )
    dec_keys = dec[0].reshape(lat_rows, nheads, HEAD)
    dec_vals = dec[1].reshape(lat_rows, nheads, HEAD)
    query = jnp.dot(enc, dq_full, preferred_element_type=jnp.float32).astype(jnp.bfloat16)
    dec_q = query.reshape(count, nheads, HEAD)
    logits = jnp.einsum("thc,lhc->htl", dec_q, dec_keys, preferred_element_type=jnp.float32) * scale
    lifted = jnp.exp(logits)
    weights = lifted / jnp.sum(lifted, axis=2, keepdims=True)
    out = jnp.einsum(
        "htl,lhc->thc", weights.astype(jnp.bfloat16), dec_vals, preferred_element_type=jnp.float32
    )
    read = readout.reshape(nheads, HEAD)
    onehot = (horizon_ids[:, None] == jnp.arange(HORIZONS, dtype=jnp.int32)[None, :]).astype(
        jnp.float32
    )
    target = jnp.sum(onehot * horizon_levels[None, :], axis=1)
    value_read = jnp.einsum("lhc,hc->hl", dec_vals.astype(jnp.float32), read, precision=high)
    lever = (
        weights
        * (
            value_read[:, None, :]
            - jnp.sum(value_read[:, None, :] * weights, axis=2, keepdims=True)
        )
    ).astype(jnp.bfloat16)
    pull = jnp.einsum("htl,lhc->thc", lever, dec_keys, preferred_element_type=jnp.float32) * scale
    field = pair_sum(jnp.sum(out * read[None, :, :], axis=(1, 2)), "heads", n_heads)
    miss = field - target
    dquery = (miss[:, None, None] * pull).reshape(count, local).astype(jnp.bfloat16)
    grad_query = lax.psum_scatter(
        jnp.dot(enc.T, dquery, preferred_element_type=jnp.float32).astype(jnp.bfloat16),
        "picks",
        scatter_dimension=0,
        tiled=True,
    ).astype(jnp.float32)
    return (field, latents_out, grad_query)


def solution(mesh):
    in_specs = (
        P(None, ("groups", "picks")),
        P(("groups", "picks")),
        P("groups"),
        P(),
        P("picks", None, "heads"),
        P("heads", None),
        P(),
        P(None, None, "heads"),
        P(None, "heads"),
        P(None, None, "heads"),
        P("picks", "heads"),
        P("heads"),
    )
    out_specs = (P(("groups", "picks")), P("groups", "heads"), P(("groups", "picks"), "heads"))
    body = functools.partial(
        on_device,
        n_picks=mesh.shape["picks"],
        n_heads=mesh.shape["heads"],
        n_groups=mesh.shape["groups"],
    )
    return jax.shard_map(body, mesh=mesh, in_specs=in_specs, out_specs=out_specs, check_vma=False)
```

```python
import functools

import jax
import jax.numpy as jnp
from jax import lax
from jax.sharding import PartitionSpec as P

HEAD = 128
BANDS = 512
HORIZONS = 64


PI = 3.141592653589793
EPS = 1e-06
RING_MAX = 4


def encode(coords):
    freq = jnp.linspace(1.0, BANDS / 2.0, BANDS).astype(jnp.float32)
    angle = PI * freq[None, :, None] * coords[:, None, :]
    table = jnp.concatenate([jnp.sin(angle), jnp.cos(angle)], axis=0)
    return table.reshape(6 * BANDS, coords.shape[1]).T.astype(jnp.bfloat16)


def ring_gather(x, axis, n):
    if n == 1:
        return x
    if n > RING_MAX:
        return lax.all_gather(x, axis, axis=0, tiled=True)
    idx = lax.axis_index(axis)
    blocks = [x]
    for s in range(1, n):
        blocks.append(lax.ppermute(x, axis, [(i, (i - s) % n) for i in range(n)]))
    flipped = jnp.stack(blocks)
    ordered = jnp.roll(flipped, idx, axis=0)
    return ordered.reshape((n * x.shape[0],) + x.shape[1:])


def fetch_rows(kv_weight, n_picks, n_groups):
    if n_groups != 2:
        return lax.all_gather(kv_weight, "picks", axis=0, tiled=True)
    g = lax.axis_index("groups")
    rows = kv_weight.shape[0] // 2
    mine = lax.dynamic_slice_in_dim(kv_weight, g * rows, rows, 0)
    first = max(8, (2 * rows // 3) // 8 * 8)
    bounds = [(0, first), (first, rows)] if first < rows else [(0, rows)]
    own, other = [], []
    for lo, hi in bounds:
        gathered = lax.all_gather(mine[lo:hi], "picks", axis=0, tiled=False)
        own.append(gathered)
        other.append(lax.ppermute(gathered, "groups", [(0, 1), (1, 0)]))
    halves = jnp.stack([jnp.concatenate(own, axis=1), jnp.concatenate(other, axis=1)], axis=1)
    halves = jnp.roll(halves, g, axis=1)
    return halves.reshape((n_picks * kv_weight.shape[0],) + kv_weight.shape[1:])


def pair_sum(x, axis, n):
    if n != 4:
        return lax.psum(x, axis)
    x = x + lax.ppermute(x, axis, [(k, k ^ 1) for k in range(n)])
    return x + lax.ppermute(x, axis, [(k, k ^ 2) for k in range(n)])


def on_device(
    coords,
    horizon_ids,
    horizon_levels,
    latents,
    kv_weight,
    cross_out,
    norm_gains,
    self_qkv,
    self_out,
    dec_kv,
    dec_query,
    readout,
    *,
    n_picks,
    n_heads,
    n_groups,
):
    high = lax.Precision.HIGHEST
    scale = HEAD ** (-0.5)
    count = coords.shape[1]
    width = latents.shape[1]
    lat_rows = latents.shape[0]
    local = kv_weight.shape[2]
    nheads = local // HEAD
    column = lax.axis_index("heads") * local
    enc = encode(coords)
    cross_full = ring_gather(cross_out, "heads", n_heads)
    piece = lax.all_gather(kv_weight, "picks", axis=0, tiled=True)
    cross_full, piece = lax.optimization_barrier((cross_full, piece))
    keys_vals = jnp.einsum(
        "tf,fjc->tjc", enc, piece, preferred_element_type=jnp.float32
    ).astype(jnp.bfloat16)
    keys = keys_vals[:, 0].reshape(count, nheads, HEAD)
    values = keys_vals[:, 1].reshape(count, nheads, HEAD)
    queries = lax.dynamic_slice_in_dim(latents, column, local, 1).reshape(lat_rows, nheads, HEAD)
    scores = jnp.einsum("lhc,thc->hlt", queries, keys, preferred_element_type=jnp.float32) * scale
    top = jnp.max(scores, axis=2)
    expo = jnp.exp(scores - top[:, :, None])
    total = jnp.sum(expo, axis=2)
    numer = jnp.einsum(
        "hlt,thc->hlc", expo.astype(jnp.bfloat16), values, preferred_element_type=jnp.float32
    )
    all_numer = lax.all_gather(numer.astype(jnp.bfloat16), "picks", axis=0, tiled=False)
    all_stats = lax.all_gather(jnp.stack([top, total]), "picks", axis=0, tiled=False)
    best = jnp.max(all_stats[:, 0], axis=0)
    factor = jnp.exp(all_stats[:, 0] - best[None])
    merged_total = jnp.sum(factor * all_stats[:, 1], axis=0)
    merged_numer = jnp.einsum(
        "phl,phlc->hlc", factor, all_numer.astype(jnp.float32), precision=high
    )
    attended = (
        (merged_numer / merged_total[:, :, None])
        .transpose(1, 0, 2)
        .reshape(lat_rows, local)
        .astype(jnp.bfloat16)
    )
    out_full = ring_gather(self_out.T, "heads", n_heads).T
    out_full, attended = lax.optimization_barrier((out_full, attended))
    dq_local, attended = lax.optimization_barrier((dec_query, attended))
    dq_full = lax.all_gather(dq_local, "picks", axis=0, tiled=True)
    attended_full = ring_gather(attended.T, "heads", n_heads).T
    whole = latents.astype(jnp.float32) + jnp.dot(
        attended_full, cross_full, preferred_element_type=jnp.float32
    )
    power = jnp.mean(whole * whole, axis=1, keepdims=True)
    normed = (whole * lax.rsqrt(power + EPS) * norm_gains[0][None, :]).astype(jnp.bfloat16)
    state = lax.dynamic_slice_in_dim(whole, column, local, 1)
    qkv = jnp.einsum("ld,kde->kle", normed, self_qkv, preferred_element_type=jnp.float32).astype(
        jnp.bfloat16
    )
    self_q = qkv[0].reshape(lat_rows, nheads, HEAD)
    self_k = qkv[1].reshape(lat_rows, nheads, HEAD)
    self_v = qkv[2].reshape(lat_rows, nheads, HEAD)
    inner = jnp.einsum("lhc,mhc->hlm", self_q, self_k, preferred_element_type=jnp.float32) * scale
    raised = jnp.exp(inner)
    probs = (raised / jnp.sum(raised, axis=2, keepdims=True)).astype(jnp.bfloat16)
    head_out = (
        jnp.einsum("hlm,mhc->lhc", probs, self_v, preferred_element_type=jnp.float32)
        .astype(jnp.bfloat16)
        .reshape(lat_rows, local)
    )
    every_head = ring_gather(head_out.T, "heads", n_heads).T
    out_whole = whole + jnp.dot(every_head, out_full, preferred_element_type=jnp.float32)
    latents_out = lax.dynamic_slice_in_dim(out_whole, column, local, 1)
    power_two = jnp.mean(out_whole * out_whole, axis=1, keepdims=True)
    normed2 = (out_whole * lax.rsqrt(power_two + EPS) * norm_gains[1][None, :]).astype(
        jnp.bfloat16
    )
    dec = jnp.einsum("ld,kde->kle", normed2, dec_kv, preferred_element_type=jnp.float32).astype(
        jnp.bfloat16
    )
    dec_keys = dec[0].reshape(lat_rows, nheads, HEAD)
    dec_vals = dec[1].reshape(lat_rows, nheads, HEAD)
    query = jnp.dot(enc, dq_full, preferred_element_type=jnp.float32).astype(jnp.bfloat16)
    dec_q = query.reshape(count, nheads, HEAD)
    logits = jnp.einsum("thc,lhc->htl", dec_q, dec_keys, preferred_element_type=jnp.float32) * scale
    lifted = jnp.exp(logits)
    weights = lifted / jnp.sum(lifted, axis=2, keepdims=True)
    out = jnp.einsum(
        "htl,lhc->thc", weights.astype(jnp.bfloat16), dec_vals, preferred_element_type=jnp.float32
    )
    read = readout.reshape(nheads, HEAD)
    onehot = (horizon_ids[:, None] == jnp.arange(HORIZONS, dtype=jnp.int32)[None, :]).astype(
        jnp.float32
    )
    target = jnp.sum(onehot * horizon_levels[None, :], axis=1)
    value_read = jnp.einsum("lhc,hc->hl", dec_vals.astype(jnp.float32), read, precision=high)
    lever = (
        weights
        * (
            value_read[:, None, :]
            - jnp.sum(value_read[:, None, :] * weights, axis=2, keepdims=True)
        )
    ).astype(jnp.bfloat16)
    pull = jnp.einsum("htl,lhc->thc", lever, dec_keys, preferred_element_type=jnp.float32) * scale
    field = pair_sum(jnp.sum(out * read[None, :, :], axis=(1, 2)), "heads", n_heads)
    miss = field - target
    dquery = (miss[:, None, None] * pull).reshape(count, local).astype(jnp.bfloat16)
    grad_query = lax.psum_scatter(
        jnp.dot(enc.T, dquery, preferred_element_type=jnp.float32).astype(jnp.bfloat16),
        "picks",
        scatter_dimension=0,
        tiled=True,
    ).astype(jnp.float32)
    return (field, latents_out, grad_query)


def solution(mesh):
    in_specs = (
        P(None, ("groups", "picks")),
        P(("groups", "picks")),
        P("groups"),
        P(),
        P("picks", None, "heads"),
        P("heads", None),
        P(),
        P(None, None, "heads"),
        P(None, "heads"),
        P(None, None, "heads"),
        P("picks", "heads"),
        P("heads"),
    )
    out_specs = (P(("groups", "picks")), P("groups", "heads"), P(("groups", "picks"), "heads"))
    body = functools.partial(
        on_device,
        n_picks=mesh.shape["picks"],
        n_heads=mesh.shape["heads"],
        n_groups=mesh.shape["groups"],
    )
    return jax.shard_map(body, mesh=mesh, in_specs=in_specs, out_specs=out_specs, check_vma=False)
```

```python
import functools

import jax
import jax.numpy as jnp
from jax import lax
from jax.sharding import PartitionSpec as P

HEAD = 128
BANDS = 512
HORIZONS = 64


PI = 3.141592653589793
EPS = 1e-06
RING_MAX = 4


def encode(coords):
    freq = jnp.linspace(1.0, BANDS / 2.0, BANDS).astype(jnp.float32)
    angle = PI * freq[None, :, None] * coords[:, None, :]
    table = jnp.concatenate([jnp.sin(angle), jnp.cos(angle)], axis=0)
    return table.reshape(6 * BANDS, coords.shape[1]).T.astype(jnp.bfloat16)


def ring_gather(x, axis, n):
    if n == 1:
        return x
    if n > RING_MAX:
        return lax.all_gather(x, axis, axis=0, tiled=True)
    idx = lax.axis_index(axis)
    blocks = [x]
    for s in range(1, n):
        blocks.append(lax.ppermute(x, axis, [(i, (i - s) % n) for i in range(n)]))
    flipped = jnp.stack(blocks)
    ordered = jnp.roll(flipped, idx, axis=0)
    return ordered.reshape((n * x.shape[0],) + x.shape[1:])


def fetch_rows(kv_weight, n_picks, n_groups):
    if n_groups != 2:
        return lax.all_gather(kv_weight, "picks", axis=0, tiled=True)
    g = lax.axis_index("groups")
    rows = kv_weight.shape[0] // 2
    mine = lax.dynamic_slice_in_dim(kv_weight, g * rows, rows, 0)
    first = max(8, (2 * rows // 3) // 8 * 8)
    bounds = [(0, first), (first, rows)] if first < rows else [(0, rows)]
    own, other = [], []
    for lo, hi in bounds:
        gathered = lax.all_gather(mine[lo:hi], "picks", axis=0, tiled=False)
        own.append(gathered)
        other.append(lax.ppermute(gathered, "groups", [(0, 1), (1, 0)]))
    halves = jnp.stack([jnp.concatenate(own, axis=1), jnp.concatenate(other, axis=1)], axis=1)
    halves = jnp.roll(halves, g, axis=1)
    return halves.reshape((n_picks * kv_weight.shape[0],) + kv_weight.shape[1:])


def pair_sum(x, axis, n):
    if n != 4:
        return lax.psum(x, axis)
    idx = lax.axis_index(axis)
    got = [x] + [lax.ppermute(x, axis, [(k, k ^ m) for k in range(n)]) for m in range(1, n)]
    terms = jnp.take(jnp.stack(got), jnp.arange(n) ^ idx, axis=0)
    return (terms[0] + terms[1]) + (terms[2] + terms[3])


def on_device(
    coords,
    horizon_ids,
    horizon_levels,
    latents,
    kv_weight,
    cross_out,
    norm_gains,
    self_qkv,
    self_out,
    dec_kv,
    dec_query,
    readout,
    *,
    n_picks,
    n_heads,
    n_groups,
):
    high = lax.Precision.HIGHEST
    scale = HEAD ** (-0.5)
    count = coords.shape[1]
    width = latents.shape[1]
    lat_rows = latents.shape[0]
    local = kv_weight.shape[2]
    nheads = local // HEAD
    column = lax.axis_index("heads") * local
    enc = encode(coords)
    cross_full = ring_gather(cross_out, "heads", n_heads)
    piece = lax.all_gather(kv_weight, "picks", axis=0, tiled=True)
    cross_full, piece = lax.optimization_barrier((cross_full, piece))
    keys_vals = jnp.einsum(
        "tf,fjc->tjc", enc, piece, preferred_element_type=jnp.float32
    ).astype(jnp.bfloat16)
    keys = keys_vals[:, 0].reshape(count, nheads, HEAD)
    values = keys_vals[:, 1].reshape(count, nheads, HEAD)
    queries = lax.dynamic_slice_in_dim(latents, column, local, 1).reshape(lat_rows, nheads, HEAD)
    scores = jnp.einsum("lhc,thc->hlt", queries, keys, preferred_element_type=jnp.float32) * scale
    top = jnp.max(scores, axis=2)
    expo = jnp.exp(scores - top[:, :, None])
    total = jnp.sum(expo, axis=2)
    numer = jnp.einsum(
        "hlt,thc->hlc", expo.astype(jnp.bfloat16), values, preferred_element_type=jnp.float32
    )
    all_numer = lax.all_gather(numer.astype(jnp.bfloat16), "picks", axis=0, tiled=False)
    all_stats = lax.all_gather(jnp.stack([top, total]), "picks", axis=0, tiled=False)
    best = jnp.max(all_stats[:, 0], axis=0)
    factor = jnp.exp(all_stats[:, 0] - best[None])
    merged_total = jnp.sum(factor * all_stats[:, 1], axis=0)
    merged_numer = jnp.einsum(
        "phl,phlc->hlc", factor, all_numer.astype(jnp.float32), precision=high
    )
    attended = (
        (merged_numer / merged_total[:, :, None])
        .transpose(1, 0, 2)
        .reshape(lat_rows, local)
        .astype(jnp.bfloat16)
    )
    out_full = ring_gather(self_out.T, "heads", n_heads).T
    out_full, attended = lax.optimization_barrier((out_full, attended))
    dq_local, attended = lax.optimization_barrier((dec_query, attended))
    dq_full = lax.all_gather(dq_local, "picks", axis=0, tiled=True)
    attended_full = ring_gather(attended.T, "heads", n_heads).T
    whole = latents.astype(jnp.float32) + jnp.dot(
        attended_full, cross_full, preferred_element_type=jnp.float32
    )
    power = jnp.mean(whole * whole, axis=1, keepdims=True)
    normed = (whole * lax.rsqrt(power + EPS) * norm_gains[0][None, :]).astype(jnp.bfloat16)
    state = lax.dynamic_slice_in_dim(whole, column, local, 1)
    qkv = jnp.einsum("ld,kde->kle", normed, self_qkv, preferred_element_type=jnp.float32).astype(
        jnp.bfloat16
    )
    self_q = qkv[0].reshape(lat_rows, nheads, HEAD)
    self_k = qkv[1].reshape(lat_rows, nheads, HEAD)
    self_v = qkv[2].reshape(lat_rows, nheads, HEAD)
    inner = jnp.einsum("lhc,mhc->hlm", self_q, self_k, preferred_element_type=jnp.float32) * scale
    raised = jnp.exp(inner)
    probs = (raised / jnp.sum(raised, axis=2, keepdims=True)).astype(jnp.bfloat16)
    head_out = (
        jnp.einsum("hlm,mhc->lhc", probs, self_v, preferred_element_type=jnp.float32)
        .astype(jnp.bfloat16)
        .reshape(lat_rows, local)
    )
    every_head = ring_gather(head_out.T, "heads", n_heads).T
    out_whole = whole + jnp.dot(every_head, out_full, preferred_element_type=jnp.float32)
    latents_out = lax.dynamic_slice_in_dim(out_whole, column, local, 1)
    power_two = jnp.mean(out_whole * out_whole, axis=1, keepdims=True)
    normed2 = (out_whole * lax.rsqrt(power_two + EPS) * norm_gains[1][None, :]).astype(
        jnp.bfloat16
    )
    dec = jnp.einsum("ld,kde->kle", normed2, dec_kv, preferred_element_type=jnp.float32).astype(
        jnp.bfloat16
    )
    dec_keys = dec[0].reshape(lat_rows, nheads, HEAD)
    dec_vals = dec[1].reshape(lat_rows, nheads, HEAD)
    query = jnp.dot(enc, dq_full, preferred_element_type=jnp.float32).astype(jnp.bfloat16)
    dec_q = query.reshape(count, nheads, HEAD)
    logits = jnp.einsum("thc,lhc->htl", dec_q, dec_keys, preferred_element_type=jnp.float32) * scale
    lifted = jnp.exp(logits)
    weights = lifted / jnp.sum(lifted, axis=2, keepdims=True)
    out = jnp.einsum(
        "htl,lhc->thc", weights.astype(jnp.bfloat16), dec_vals, preferred_element_type=jnp.float32
    )
    read = readout.reshape(nheads, HEAD)
    onehot = (horizon_ids[:, None] == jnp.arange(HORIZONS, dtype=jnp.int32)[None, :]).astype(
        jnp.float32
    )
    target = jnp.sum(onehot * horizon_levels[None, :], axis=1)
    value_read = jnp.einsum("lhc,hc->hl", dec_vals.astype(jnp.float32), read, precision=high)
    lever = (
        weights
        * (
            value_read[:, None, :]
            - jnp.sum(value_read[:, None, :] * weights, axis=2, keepdims=True)
        )
    ).astype(jnp.bfloat16)
    pull = jnp.einsum("htl,lhc->thc", lever, dec_keys, preferred_element_type=jnp.float32) * scale
    field = pair_sum(jnp.sum(out * read[None, :, :], axis=(1, 2)), "heads", n_heads)
    miss = field - target
    dquery = (miss[:, None, None] * pull).reshape(count, local).astype(jnp.bfloat16)
    grad_query = lax.psum_scatter(
        jnp.dot(enc.T, dquery, preferred_element_type=jnp.float32).astype(jnp.bfloat16),
        "picks",
        scatter_dimension=0,
        tiled=True,
    ).astype(jnp.float32)
    return (field, latents_out, grad_query)


def solution(mesh):
    in_specs = (
        P(None, ("groups", "picks")),
        P(("groups", "picks")),
        P("groups"),
        P(),
        P("picks", None, "heads"),
        P("heads", None),
        P(),
        P(None, None, "heads"),
        P(None, "heads"),
        P(None, None, "heads"),
        P("picks", "heads"),
        P("heads"),
    )
    out_specs = (P(("groups", "picks")), P("groups", "heads"), P(("groups", "picks"), "heads"))
    body = functools.partial(
        on_device,
        n_picks=mesh.shape["picks"],
        n_heads=mesh.shape["heads"],
        n_groups=mesh.shape["groups"],
    )
    return jax.shard_map(body, mesh=mesh, in_specs=in_specs, out_specs=out_specs, check_vma=False)
```

```python
import functools

import jax
import jax.numpy as jnp
from jax import lax
from jax.sharding import PartitionSpec as P

HEAD = 128
BANDS = 512
HORIZONS = 64


PI = 3.141592653589793
EPS = 1e-06
RING_MAX = 4


def encode(coords):
    freq = jnp.linspace(1.0, BANDS / 2.0, BANDS).astype(jnp.float32)
    angle = PI * freq[None, :, None] * coords[:, None, :]
    table = jnp.concatenate([jnp.sin(angle), jnp.cos(angle)], axis=0)
    return table.reshape(6 * BANDS, coords.shape[1]).T.astype(jnp.bfloat16)


def ring_gather(x, axis, n):
    if n == 1:
        return x
    if n > RING_MAX:
        return lax.all_gather(x, axis, axis=0, tiled=True)
    idx = lax.axis_index(axis)
    blocks = [x]
    for s in range(1, n):
        blocks.append(lax.ppermute(x, axis, [(i, (i - s) % n) for i in range(n)]))
    flipped = jnp.stack(blocks)
    ordered = jnp.roll(flipped, idx, axis=0)
    return ordered.reshape((n * x.shape[0],) + x.shape[1:])


def fetch_rows(kv_weight, n_picks, n_groups):
    if n_groups != 2:
        return lax.all_gather(kv_weight, "picks", axis=0, tiled=True)
    g = lax.axis_index("groups")
    rows = kv_weight.shape[0] // 2
    mine = lax.dynamic_slice_in_dim(kv_weight, g * rows, rows, 0)
    first = max(8, (2 * rows // 3) // 8 * 8)
    bounds = [(0, first), (first, rows)] if first < rows else [(0, rows)]
    own, other = [], []
    for lo, hi in bounds:
        gathered = lax.all_gather(mine[lo:hi], "picks", axis=0, tiled=False)
        own.append(gathered)
        other.append(lax.ppermute(gathered, "groups", [(0, 1), (1, 0)]))
    halves = jnp.stack([jnp.concatenate(own, axis=1), jnp.concatenate(other, axis=1)], axis=1)
    halves = jnp.roll(halves, g, axis=1)
    return halves.reshape((n_picks * kv_weight.shape[0],) + kv_weight.shape[1:])


def pair_sum(x, axis, n):
    if n != 4:
        return lax.psum(x, axis)
    x = x + lax.ppermute(x, axis, [(k, k ^ 1) for k in range(n)])
    return x + lax.ppermute(x, axis, [(k, k ^ 2) for k in range(n)])


def on_device(
    coords,
    horizon_ids,
    horizon_levels,
    latents,
    kv_weight,
    cross_out,
    norm_gains,
    self_qkv,
    self_out,
    dec_kv,
    dec_query,
    readout,
    *,
    n_picks,
    n_heads,
    n_groups,
):
    high = lax.Precision.HIGHEST
    scale = HEAD ** (-0.5)
    count = coords.shape[1]
    width = latents.shape[1]
    lat_rows = latents.shape[0]
    local = kv_weight.shape[2]
    nheads = local // HEAD
    column = lax.axis_index("heads") * local
    enc = encode(coords)
    cross_full = ring_gather(cross_out, "heads", n_heads)
    piece = lax.all_gather(kv_weight, "picks", axis=0, tiled=True)
    cross_full, piece = lax.optimization_barrier((cross_full, piece))
    keys_vals = jnp.einsum(
        "tf,fjc->tjc", enc, piece, preferred_element_type=jnp.float32
    ).astype(jnp.bfloat16)
    keys = keys_vals[:, 0].reshape(count, nheads, HEAD)
    values = keys_vals[:, 1].reshape(count, nheads, HEAD)
    queries = lax.dynamic_slice_in_dim(latents, column, local, 1).reshape(lat_rows, nheads, HEAD)
    scores = jnp.einsum("lhc,thc->hlt", queries, keys, preferred_element_type=jnp.float32) * scale
    top = jnp.max(scores, axis=2)
    expo = jnp.exp(scores - top[:, :, None])
    total = jnp.sum(expo, axis=2)
    numer = jnp.einsum(
        "hlt,thc->hlc", expo.astype(jnp.bfloat16), values, preferred_element_type=jnp.float32
    )
    all_numer = lax.all_gather(numer.astype(jnp.bfloat16), "picks", axis=0, tiled=False)
    all_stats = lax.all_gather(jnp.stack([top, total]), "picks", axis=0, tiled=False)
    best = jnp.max(all_stats[:, 0], axis=0)
    factor = jnp.exp(all_stats[:, 0] - best[None])
    merged_total = jnp.sum(factor * all_stats[:, 1], axis=0)
    merged_numer = jnp.einsum(
        "phl,phlc->hlc", factor, all_numer.astype(jnp.float32), precision=high
    )
    attended = (
        (merged_numer / merged_total[:, :, None])
        .transpose(1, 0, 2)
        .reshape(lat_rows, local)
        .astype(jnp.bfloat16)
    )
    out_full = ring_gather(self_out.T, "heads", n_heads).T
    out_full, attended = lax.optimization_barrier((out_full, attended))
    dq_local, attended = lax.optimization_barrier((dec_query, attended))
    dq_full = lax.all_gather(dq_local, "picks", axis=0, tiled=True)
    attended_full = ring_gather(attended.T, "heads", n_heads).T
    whole = latents.astype(jnp.float32) + jnp.dot(
        attended_full, cross_full, preferred_element_type=jnp.float32
    )
    power = jnp.mean(whole * whole, axis=1, keepdims=True)
    normed = (whole * lax.rsqrt(power + EPS) * norm_gains[0][None, :]).astype(jnp.bfloat16)
    state = lax.dynamic_slice_in_dim(whole, column, local, 1)
    qkv = jnp.einsum("ld,kde->kle", normed, self_qkv, preferred_element_type=jnp.float32).astype(
        jnp.bfloat16
    )
    self_q = qkv[0].reshape(lat_rows, nheads, HEAD)
    self_k = qkv[1].reshape(lat_rows, nheads, HEAD)
    self_v = qkv[2].reshape(lat_rows, nheads, HEAD)
    inner = jnp.einsum("lhc,mhc->hlm", self_q, self_k, preferred_element_type=jnp.float32) * scale
    raised = jnp.exp(inner)
    probs = (raised / jnp.sum(raised, axis=2, keepdims=True)).astype(jnp.bfloat16)
    head_out = (
        jnp.einsum("hlm,mhc->lhc", probs, self_v, preferred_element_type=jnp.float32)
        .astype(jnp.bfloat16)
        .reshape(lat_rows, local)
    )
    every_head = ring_gather(head_out.T, "heads", n_heads).T
    out_whole = whole + jnp.dot(every_head, out_full, preferred_element_type=jnp.float32)
    latents_out = lax.dynamic_slice_in_dim(out_whole, column, local, 1)
    power_two = jnp.mean(out_whole * out_whole, axis=1, keepdims=True)
    normed2 = (out_whole * lax.rsqrt(power_two + EPS) * norm_gains[1][None, :]).astype(
        jnp.bfloat16
    )
    dec = jnp.einsum("ld,kde->kle", normed2, dec_kv, preferred_element_type=jnp.float32).astype(
        jnp.bfloat16
    )
    dec_keys = dec[0].reshape(lat_rows, nheads, HEAD)
    dec_vals = dec[1].reshape(lat_rows, nheads, HEAD)
    query = jnp.dot(enc, dq_full, preferred_element_type=jnp.float32).astype(jnp.bfloat16)
    dec_q = query.reshape(count, nheads, HEAD)
    logits = jnp.einsum("thc,lhc->htl", dec_q, dec_keys, preferred_element_type=jnp.float32) * scale
    lifted = jnp.exp(logits)
    weights = lifted / jnp.sum(lifted, axis=2, keepdims=True)
    out = jnp.einsum(
        "htl,lhc->thc", weights.astype(jnp.bfloat16), dec_vals, preferred_element_type=jnp.float32
    )
    read = readout.reshape(nheads, HEAD)
    onehot = (horizon_ids[:, None] == jnp.arange(HORIZONS, dtype=jnp.int32)[None, :]).astype(
        jnp.float32
    )
    target = jnp.sum(onehot * horizon_levels[None, :], axis=1)
    value_read = jnp.einsum("lhc,hc->hl", dec_vals.astype(jnp.float32), read, precision=high)
    lever = (
        weights
        * (
            value_read[:, None, :]
            - jnp.sum(value_read[:, None, :] * weights, axis=2, keepdims=True)
        )
    ).astype(jnp.bfloat16)
    pull = jnp.einsum("htl,lhc->thc", lever, dec_keys, preferred_element_type=jnp.float32) * scale
    field = pair_sum(jnp.sum(out * read[None, :, :], axis=(1, 2)), "heads", n_heads)
    miss = field - target
    dquery = (miss[:, None, None] * pull).reshape(count, local).astype(jnp.bfloat16)
    grad_query = (
        lax.psum_scatter(
            jnp.dot(dquery.T, enc, preferred_element_type=jnp.float32).astype(jnp.bfloat16),
            "picks",
            scatter_dimension=1,
            tiled=True,
        )
        .astype(jnp.float32)
        .T
    )
    return (field, latents_out, grad_query)


def solution(mesh):
    in_specs = (
        P(None, ("groups", "picks")),
        P(("groups", "picks")),
        P("groups"),
        P(),
        P("picks", None, "heads"),
        P("heads", None),
        P(),
        P(None, None, "heads"),
        P(None, "heads"),
        P(None, None, "heads"),
        P("picks", "heads"),
        P("heads"),
    )
    out_specs = (P(("groups", "picks")), P("groups", "heads"), P(("groups", "picks"), "heads"))
    body = functools.partial(
        on_device,
        n_picks=mesh.shape["picks"],
        n_heads=mesh.shape["heads"],
        n_groups=mesh.shape["groups"],
    )
    return jax.shard_map(body, mesh=mesh, in_specs=in_specs, out_specs=out_specs, check_vma=False)
```

```python
import functools

import jax
import jax.numpy as jnp
from jax import lax
from jax.sharding import PartitionSpec as P

HEAD = 128
BANDS = 512
HORIZONS = 64


PI = 3.141592653589793
EPS = 1e-06
RING_MAX = 4


def encode(coords):
    freq = jnp.linspace(1.0, BANDS / 2.0, BANDS).astype(jnp.float32)
    angle = PI * freq[None, :, None] * coords[:, None, :]
    table = jnp.concatenate([jnp.sin(angle), jnp.cos(angle)], axis=0)
    return table.reshape(6 * BANDS, coords.shape[1]).T.astype(jnp.bfloat16)


def ring_gather(x, axis, n):
    if n == 1:
        return x
    if n > RING_MAX:
        return lax.all_gather(x, axis, axis=0, tiled=True)
    idx = lax.axis_index(axis)
    blocks = [x]
    for s in range(1, n):
        blocks.append(lax.ppermute(x, axis, [(i, (i - s) % n) for i in range(n)]))
    flipped = jnp.stack(blocks)
    ordered = jnp.roll(flipped, idx, axis=0)
    return ordered.reshape((n * x.shape[0],) + x.shape[1:])


def fetch_rows(kv_weight, n_picks, n_groups):
    if n_groups != 2:
        return lax.all_gather(kv_weight, "picks", axis=0, tiled=True)
    g = lax.axis_index("groups")
    rows = kv_weight.shape[0] // 2
    mine = lax.dynamic_slice_in_dim(kv_weight, g * rows, rows, 0)
    first = max(8, (2 * rows // 3) // 8 * 8)
    bounds = [(0, first), (first, rows)] if first < rows else [(0, rows)]
    own, other = [], []
    for lo, hi in bounds:
        gathered = lax.all_gather(mine[lo:hi], "picks", axis=0, tiled=False)
        own.append(gathered)
        other.append(lax.ppermute(gathered, "groups", [(0, 1), (1, 0)]))
    halves = jnp.stack([jnp.concatenate(own, axis=1), jnp.concatenate(other, axis=1)], axis=1)
    halves = jnp.roll(halves, g, axis=1)
    return halves.reshape((n_picks * kv_weight.shape[0],) + kv_weight.shape[1:])


def pair_sum(x, axis, n):
    if n != 4:
        return lax.psum(x, axis)
    x = x + lax.ppermute(x, axis, [(k, k ^ 1) for k in range(n)])
    return x + lax.ppermute(x, axis, [(k, k ^ 2) for k in range(n)])


def pair_gather(x, axis, n):
    near = lax.ppermute(x, axis, [(k, k ^ 1) for k in range(n)])
    far = lax.ppermute(x, axis, [(k, k ^ 2) for k in range(n)])
    far_near = lax.ppermute(far, axis, [(k, k ^ 1) for k in range(n)])
    return jnp.concatenate([x, near, far, far_near], axis=0)


def xor_blocks(x, idx, n):
    blocks = x.reshape((n, x.shape[0] // n) + x.shape[1:])
    return jnp.take(blocks, jnp.arange(n) ^ idx, axis=0).reshape(x.shape)


def on_device(
    coords,
    horizon_ids,
    horizon_levels,
    latents,
    kv_weight,
    cross_out,
    norm_gains,
    self_qkv,
    self_out,
    dec_kv,
    dec_query,
    readout,
    *,
    n_picks,
    n_heads,
    n_groups,
):
    high = lax.Precision.HIGHEST
    scale = HEAD ** (-0.5)
    count = coords.shape[1]
    width = latents.shape[1]
    lat_rows = latents.shape[0]
    local = kv_weight.shape[2]
    nheads = local // HEAD
    column = lax.axis_index("heads") * local
    enc = encode(coords)
    cross_full = ring_gather(cross_out, "heads", n_heads)
    piece = lax.all_gather(kv_weight, "picks", axis=0, tiled=True)
    paired = n_heads == 4
    out_full = ring_gather(self_out.T, "heads", n_heads).T
    if paired:
        out_full = xor_blocks(out_full, lax.axis_index("heads"), n_heads)
    out_full, cross_full, piece = lax.optimization_barrier((out_full, cross_full, piece))
    keys_vals = jnp.einsum(
        "tf,fjc->tjc", enc, piece, preferred_element_type=jnp.float32
    ).astype(jnp.bfloat16)
    keys = keys_vals[:, 0].reshape(count, nheads, HEAD)
    values = keys_vals[:, 1].reshape(count, nheads, HEAD)
    queries = lax.dynamic_slice_in_dim(latents, column, local, 1).reshape(lat_rows, nheads, HEAD)
    scores = jnp.einsum("lhc,thc->hlt", queries, keys, preferred_element_type=jnp.float32) * scale
    top = jnp.max(scores, axis=2)
    expo = jnp.exp(scores - top[:, :, None])
    total = jnp.sum(expo, axis=2)
    numer = jnp.einsum(
        "hlt,thc->hlc", expo.astype(jnp.bfloat16), values, preferred_element_type=jnp.float32
    )
    all_numer = lax.all_gather(numer.astype(jnp.bfloat16), "picks", axis=0, tiled=False)
    all_stats = lax.all_gather(jnp.stack([top, total]), "picks", axis=0, tiled=False)
    best = jnp.max(all_stats[:, 0], axis=0)
    factor = jnp.exp(all_stats[:, 0] - best[None])
    merged_total = jnp.sum(factor * all_stats[:, 1], axis=0)
    merged_numer = jnp.einsum(
        "phl,phlc->hlc", factor, all_numer.astype(jnp.float32), precision=high
    )
    attended = (
        (merged_numer / merged_total[:, :, None])
        .transpose(1, 0, 2)
        .reshape(lat_rows, local)
        .astype(jnp.bfloat16)
    )
    dq_local, attended = lax.optimization_barrier((dec_query, attended))
    dq_full = lax.all_gather(dq_local, "picks", axis=0, tiled=True)
    attended_full = ring_gather(attended.T, "heads", n_heads).T
    whole = latents.astype(jnp.float32) + jnp.dot(
        attended_full, cross_full, preferred_element_type=jnp.float32
    )
    power = jnp.mean(whole * whole, axis=1, keepdims=True)
    normed = (whole * lax.rsqrt(power + EPS) * norm_gains[0][None, :]).astype(jnp.bfloat16)
    state = lax.dynamic_slice_in_dim(whole, column, local, 1)
    qkv = jnp.einsum("ld,kde->kle", normed, self_qkv, preferred_element_type=jnp.float32).astype(
        jnp.bfloat16
    )
    self_q = qkv[0].reshape(lat_rows, nheads, HEAD)
    self_k = qkv[1].reshape(lat_rows, nheads, HEAD)
    self_v = qkv[2].reshape(lat_rows, nheads, HEAD)
    inner = jnp.einsum("lhc,mhc->hlm", self_q, self_k, preferred_element_type=jnp.float32) * scale
    raised = jnp.exp(inner)
    probs = (raised / jnp.sum(raised, axis=2, keepdims=True)).astype(jnp.bfloat16)
    head_out = (
        jnp.einsum("hlm,mhc->lhc", probs, self_v, preferred_element_type=jnp.float32)
        .astype(jnp.bfloat16)
        .reshape(lat_rows, local)
    )
    head_gather = pair_gather if paired else ring_gather
    every_head = head_gather(head_out.T, "heads", n_heads).T
    out_whole = whole + jnp.dot(every_head, out_full, preferred_element_type=jnp.float32)
    latents_out = lax.dynamic_slice_in_dim(out_whole, column, local, 1)
    power_two = jnp.mean(out_whole * out_whole, axis=1, keepdims=True)
    normed2 = (out_whole * lax.rsqrt(power_two + EPS) * norm_gains[1][None, :]).astype(
        jnp.bfloat16
    )
    dec = jnp.einsum("ld,kde->kle", normed2, dec_kv, preferred_element_type=jnp.float32).astype(
        jnp.bfloat16
    )
    dec_keys = dec[0].reshape(lat_rows, nheads, HEAD)
    dec_vals = dec[1].reshape(lat_rows, nheads, HEAD)
    query = jnp.dot(enc, dq_full, preferred_element_type=jnp.float32).astype(jnp.bfloat16)
    dec_q = query.reshape(count, nheads, HEAD)
    logits = jnp.einsum("thc,lhc->htl", dec_q, dec_keys, preferred_element_type=jnp.float32) * scale
    lifted = jnp.exp(logits)
    weights = lifted / jnp.sum(lifted, axis=2, keepdims=True)
    out = jnp.einsum(
        "htl,lhc->thc", weights.astype(jnp.bfloat16), dec_vals, preferred_element_type=jnp.float32
    )
    read = readout.reshape(nheads, HEAD)
    onehot = (horizon_ids[:, None] == jnp.arange(HORIZONS, dtype=jnp.int32)[None, :]).astype(
        jnp.float32
    )
    target = jnp.sum(onehot * horizon_levels[None, :], axis=1)
    value_read = jnp.einsum("lhc,hc->hl", dec_vals.astype(jnp.float32), read, precision=high)
    lever = (
        weights
        * (
            value_read[:, None, :]
            - jnp.sum(value_read[:, None, :] * weights, axis=2, keepdims=True)
        )
    ).astype(jnp.bfloat16)
    pull = jnp.einsum("htl,lhc->thc", lever, dec_keys, preferred_element_type=jnp.float32) * scale
    field = pair_sum(jnp.sum(out * read[None, :, :], axis=(1, 2)), "heads", n_heads)
    miss = field - target
    dquery = (miss[:, None, None] * pull).reshape(count, local).astype(jnp.bfloat16)
    grad_query = lax.psum_scatter(
        jnp.dot(enc.T, dquery, preferred_element_type=jnp.float32).astype(jnp.bfloat16),
        "picks",
        scatter_dimension=0,
        tiled=True,
    ).astype(jnp.float32)
    return (field, latents_out, grad_query)


def solution(mesh):
    in_specs = (
        P(None, ("groups", "picks")),
        P(("groups", "picks")),
        P("groups"),
        P(),
        P("picks", None, "heads"),
        P("heads", None),
        P(),
        P(None, None, "heads"),
        P(None, "heads"),
        P(None, None, "heads"),
        P("picks", "heads"),
        P("heads"),
    )
    out_specs = (P(("groups", "picks")), P("groups", "heads"), P(("groups", "picks"), "heads"))
    body = functools.partial(
        on_device,
        n_picks=mesh.shape["picks"],
        n_heads=mesh.shape["heads"],
        n_groups=mesh.shape["groups"],
    )
    return jax.shard_map(body, mesh=mesh, in_specs=in_specs, out_specs=out_specs, check_vma=False)
```

```python
import functools

import jax
import jax.numpy as jnp
from jax import lax
from jax.sharding import PartitionSpec as P

HEAD = 128
BANDS = 512
HORIZONS = 64


PI = 3.141592653589793
EPS = 1e-06
RING_MAX = 4


def encode(coords):
    freq = jnp.linspace(1.0, BANDS / 2.0, BANDS).astype(jnp.float32)
    angle = PI * freq[None, :, None] * coords[:, None, :]
    table = jnp.concatenate([jnp.sin(angle), jnp.cos(angle)], axis=0)
    return table.reshape(6 * BANDS, coords.shape[1]).T.astype(jnp.bfloat16)


def ring_gather(x, axis, n):
    if n == 1:
        return x
    if n > RING_MAX:
        return lax.all_gather(x, axis, axis=0, tiled=True)
    idx = lax.axis_index(axis)
    blocks = [x]
    for s in range(1, n):
        blocks.append(lax.ppermute(x, axis, [(i, (i - s) % n) for i in range(n)]))
    flipped = jnp.stack(blocks)
    ordered = jnp.roll(flipped, idx, axis=0)
    return ordered.reshape((n * x.shape[0],) + x.shape[1:])


def fetch_rows(kv_weight, n_picks, n_groups):
    if n_groups != 2:
        return lax.all_gather(kv_weight, "picks", axis=0, tiled=True)
    g = lax.axis_index("groups")
    rows = kv_weight.shape[0] // 2
    mine = lax.dynamic_slice_in_dim(kv_weight, g * rows, rows, 0)
    first = max(8, (2 * rows // 3) // 8 * 8)
    bounds = [(0, first), (first, rows)] if first < rows else [(0, rows)]
    own, other = [], []
    for lo, hi in bounds:
        gathered = lax.all_gather(mine[lo:hi], "picks", axis=0, tiled=False)
        own.append(gathered)
        other.append(lax.ppermute(gathered, "groups", [(0, 1), (1, 0)]))
    halves = jnp.stack([jnp.concatenate(own, axis=1), jnp.concatenate(other, axis=1)], axis=1)
    halves = jnp.roll(halves, g, axis=1)
    return halves.reshape((n_picks * kv_weight.shape[0],) + kv_weight.shape[1:])


def pair_sum(x, axis, n):
    if n != 4:
        return lax.psum(x, axis)
    x = x + lax.ppermute(x, axis, [(k, k ^ 1) for k in range(n)])
    return x + lax.ppermute(x, axis, [(k, k ^ 2) for k in range(n)])


def on_device(
    coords,
    horizon_ids,
    horizon_levels,
    latents,
    kv_weight,
    cross_out,
    norm_gains,
    self_qkv,
    self_out,
    dec_kv,
    dec_query,
    readout,
    *,
    n_picks,
    n_heads,
    n_groups,
):
    high = lax.Precision.HIGHEST
    scale = HEAD ** (-0.5)
    count = coords.shape[1]
    width = latents.shape[1]
    lat_rows = latents.shape[0]
    local = kv_weight.shape[2]
    nheads = local // HEAD
    column = lax.axis_index("heads") * local
    enc = encode(coords)
    cross_full = ring_gather(cross_out, "heads", n_heads)
    piece = lax.all_gather(kv_weight, "picks", axis=0, tiled=True)
    cross_full, piece = lax.optimization_barrier((cross_full, piece))
    keys_vals = jnp.einsum(
        "tf,fjc->tjc", enc, piece, preferred_element_type=jnp.float32
    ).astype(jnp.bfloat16)
    keys = keys_vals[:, 0].reshape(count, nheads, HEAD)
    values = keys_vals[:, 1].reshape(count, nheads, HEAD)
    queries = lax.dynamic_slice_in_dim(latents, column, local, 1).reshape(lat_rows, nheads, HEAD)
    scores = jnp.einsum("lhc,thc->hlt", queries, keys, preferred_element_type=jnp.float32) * scale
    top = jnp.max(scores, axis=2)
    expo = jnp.exp(scores - top[:, :, None])
    total = jnp.sum(expo, axis=2)
    numer = jnp.einsum(
        "hlt,thc->hlc", expo.astype(jnp.bfloat16), values, preferred_element_type=jnp.float32
    )
    part = numer.astype(jnp.bfloat16)
    all_numer = ring_gather(part[None], "picks", n_picks)
    all_stats = lax.all_gather(jnp.stack([top, total]), "picks", axis=0, tiled=False)
    best = jnp.max(all_stats[:, 0], axis=0)
    factor = jnp.exp(all_stats[:, 0] - best[None])
    merged_total = jnp.sum(factor * all_stats[:, 1], axis=0)
    merged_numer = jnp.einsum(
        "phl,phlc->hlc", factor, all_numer.astype(jnp.float32), precision=high
    )
    attended = (
        (merged_numer / merged_total[:, :, None])
        .transpose(1, 0, 2)
        .reshape(lat_rows, local)
        .astype(jnp.bfloat16)
    )
    out_full = ring_gather(self_out.T, "heads", n_heads).T
    out_full, attended = lax.optimization_barrier((out_full, attended))
    dq_local, attended = lax.optimization_barrier((dec_query, attended))
    dq_full = lax.all_gather(dq_local, "picks", axis=0, tiled=True)
    attended_full = ring_gather(attended.T, "heads", n_heads).T
    whole = latents.astype(jnp.float32) + jnp.dot(
        attended_full, cross_full, preferred_element_type=jnp.float32
    )
    power = jnp.mean(whole * whole, axis=1, keepdims=True)
    normed = (whole * lax.rsqrt(power + EPS) * norm_gains[0][None, :]).astype(jnp.bfloat16)
    state = lax.dynamic_slice_in_dim(whole, column, local, 1)
    qkv = jnp.einsum("ld,kde->kle", normed, self_qkv, preferred_element_type=jnp.float32).astype(
        jnp.bfloat16
    )
    self_q = qkv[0].reshape(lat_rows, nheads, HEAD)
    self_k = qkv[1].reshape(lat_rows, nheads, HEAD)
    self_v = qkv[2].reshape(lat_rows, nheads, HEAD)
    inner = jnp.einsum("lhc,mhc->hlm", self_q, self_k, preferred_element_type=jnp.float32) * scale
    raised = jnp.exp(inner)
    probs = (raised / jnp.sum(raised, axis=2, keepdims=True)).astype(jnp.bfloat16)
    head_out = (
        jnp.einsum("hlm,mhc->lhc", probs, self_v, preferred_element_type=jnp.float32)
        .astype(jnp.bfloat16)
        .reshape(lat_rows, local)
    )
    every_head = ring_gather(head_out.T, "heads", n_heads).T
    out_whole = whole + jnp.dot(every_head, out_full, preferred_element_type=jnp.float32)
    latents_out = lax.dynamic_slice_in_dim(out_whole, column, local, 1)
    power_two = jnp.mean(out_whole * out_whole, axis=1, keepdims=True)
    normed2 = (out_whole * lax.rsqrt(power_two + EPS) * norm_gains[1][None, :]).astype(
        jnp.bfloat16
    )
    dec = jnp.einsum("ld,kde->kle", normed2, dec_kv, preferred_element_type=jnp.float32).astype(
        jnp.bfloat16
    )
    dec_keys = dec[0].reshape(lat_rows, nheads, HEAD)
    dec_vals = dec[1].reshape(lat_rows, nheads, HEAD)
    query = jnp.dot(enc, dq_full, preferred_element_type=jnp.float32).astype(jnp.bfloat16)
    dec_q = query.reshape(count, nheads, HEAD)
    logits = jnp.einsum("thc,lhc->htl", dec_q, dec_keys, preferred_element_type=jnp.float32) * scale
    lifted = jnp.exp(logits)
    weights = lifted / jnp.sum(lifted, axis=2, keepdims=True)
    out = jnp.einsum(
        "htl,lhc->thc", weights.astype(jnp.bfloat16), dec_vals, preferred_element_type=jnp.float32
    )
    read = readout.reshape(nheads, HEAD)
    onehot = (horizon_ids[:, None] == jnp.arange(HORIZONS, dtype=jnp.int32)[None, :]).astype(
        jnp.float32
    )
    target = jnp.sum(onehot * horizon_levels[None, :], axis=1)
    value_read = jnp.einsum("lhc,hc->hl", dec_vals.astype(jnp.float32), read, precision=high)
    lever = (
        weights
        * (
            value_read[:, None, :]
            - jnp.sum(value_read[:, None, :] * weights, axis=2, keepdims=True)
        )
    ).astype(jnp.bfloat16)
    pull = jnp.einsum("htl,lhc->thc", lever, dec_keys, preferred_element_type=jnp.float32) * scale
    field = pair_sum(jnp.sum(out * read[None, :, :], axis=(1, 2)), "heads", n_heads)
    miss = field - target
    dquery = (miss[:, None, None] * pull).reshape(count, local).astype(jnp.bfloat16)
    grad_query = lax.psum_scatter(
        jnp.dot(enc.T, dquery, preferred_element_type=jnp.float32).astype(jnp.bfloat16),
        "picks",
        scatter_dimension=0,
        tiled=True,
    ).astype(jnp.float32)
    return (field, latents_out, grad_query)


def solution(mesh):
    in_specs = (
        P(None, ("groups", "picks")),
        P(("groups", "picks")),
        P("groups"),
        P(),
        P("picks", None, "heads"),
        P("heads", None),
        P(),
        P(None, None, "heads"),
        P(None, "heads"),
        P(None, None, "heads"),
        P("picks", "heads"),
        P("heads"),
    )
    out_specs = (P(("groups", "picks")), P("groups", "heads"), P(("groups", "picks"), "heads"))
    body = functools.partial(
        on_device,
        n_picks=mesh.shape["picks"],
        n_heads=mesh.shape["heads"],
        n_groups=mesh.shape["groups"],
    )
    return jax.shard_map(body, mesh=mesh, in_specs=in_specs, out_specs=out_specs, check_vma=False)
```
